32 devices in a mesh: row: 4 (over x, core), col: 8 (over z, y).
Axes of the slice: x: 2, y: 2, z: 4, core: 2. Of those that a mesh axis runs over, the one named last changes fastest.
Arguments:
- atom_feat: float32 [8192, 128], P(('row', 'col')), may hold values from -6 to 6
- types: int32 [8192], P(('row', 'col')), may hold values from 0 to 3
- neighbors: int32 [8192, 32], P(('row', 'col')), may hold values from 0 to 255
- frame_of_atom: int32 [8192], P(('row', 'col')), may hold values from 0 to 3
- weights: float32 [128, 128], replicated, may hold values from -0.5 to 0.5
- type_gain: float32 [4, 128], replicated, may hold values from -4 to 4
- out_vec: float32 [4, 128], replicated, may hold values from -1.5 to 1.5
- targets: float32 [128], replicated, may hold values from -5 to 5
- noise: float32 [128], replicated, may hold values from 0.05 to 2
- cov: float32 [16384, 16384], P('row', 'col'), as said below
Outputs:
- new_weights: float32 [16384], P(('row', 'col'))
- new_cov: float32 [16384, 16384], P('row', 'col')
The draws below stay inside these ranges and needn't reach their ends.
Inputs may be any that keep to these rules, and one draw needn't show every extreme that they name: cov is symmetric positive definite.
All inputs are finite; a program needn't handle non-finite values.
Results may differ from the reference program's by a relative error of at most 0.0003.
Values sent between devices are 32-bit elements; how exact they have to be, the bound alone decides.
No kernel may reach another device: no remote copies, remote signals or barrier semaphores. Data moves between devices by JAX's collectives and lax.ppermute only.
A program may use at most 192 MiB of HBM per device.

```python
import math
import jax
import jax.numpy as jnp
from jax import lax

NI = 128
NO = 128
NT = 4
NB = 32
FR = 64
ATOM_DEV = 256
NW = 16384
ATOMS = 8192
M = 128
N_ROW = 4
N_COL = 8


def draw_cov(key, part):
    first, second, third = jax.random.split(key, 3)
    points = jax.random.uniform(first, (NW, 3), jnp.float32)
    reach = (16.0 / NW) ** (1.0 / 3.0)
    diag = jax.random.uniform(second, (NW,), jnp.float32, 2.0, 4.0)
    scales = jax.random.uniform(third, (NW,), jnp.float32, 0.7, 1.3)
    dist = jnp.abs(points[:, None, 0] - points[None, :, 0])
    dist = dist + jnp.abs(points[:, None, 1] - points[None, :, 1])
    dist = dist + jnp.abs(points[:, None, 2] - points[None, :, 2])
    kernel = scales[:, None] * scales[None, :] * jnp.exp(-dist / reach)
    return kernel + jnp.diag(diag)


def with_ends(array, rng, least, top_value):
    extent = array.shape
    spot = [jax.random.randint(jax.random.fold_in(rng, axis), (), 0, extent[axis]) for axis in range(len(extent))]
    array = array.at[tuple(spot)].set(least)
    longest = extent.index(max(extent))
    spot[longest] = (spot[longest] + 1) % extent[longest]
    return array.at[tuple(spot)].set(top_value)


def steps_of(own_key, extent, shards, smallest, largest):
    gain = 1.0
    for axis_at, parts in shards:
        heights = jax.random.uniform(jax.random.fold_in(jax.random.fold_in(own_key, 6), axis_at), (parts,), jnp.float32, smallest / len(shards), largest / len(shards))
        gain = gain * jnp.repeat(jnp.exp(heights), extent[axis_at] // parts).reshape((-1,) + (1,) * (len(extent) - 1 - axis_at))
    return gain


def bell_draw(key, shape, scale, most, shards=(), kind=jnp.bfloat16):
    result = jax.random.normal(key, shape, jnp.float32) * scale
    if len(shards) > 0:
        result = steps_of(key, shape, shards, -0.22, 0.18) * result
    return jnp.clip(result, min=-most, max=most).astype(kind)


def setup_inputs(seed: int = 0) -> dict:
    key_list = jax.random.split(jax.random.key(seed), 11)
    return {
        "atom_feat": bell_draw(key_list[0], (ATOMS, NI), 1.0, 6.0, ((0, 32),), jnp.float32),
        "types": with_ends(jax.random.randint(key_list[1], (ATOMS,), 0, NT), jax.random.fold_in(key_list[1], 1), 0, NT - 1).astype(jnp.int32),
        "neighbors": with_ends(jax.random.randint(key_list[2], (ATOMS, NB), 0, ATOM_DEV), jax.random.fold_in(key_list[2], 1), 0, ATOM_DEV - 1).astype(jnp.int32),
        "frame_of_atom": with_ends(jax.random.randint(key_list[3], (ATOMS,), 0, ATOM_DEV // FR), jax.random.fold_in(key_list[3], 1), 0, (ATOM_DEV // FR) - 1).astype(jnp.int32),
        "weights": bell_draw(key_list[4], (NI, NO), NI ** -0.5, 0.5, (), jnp.float32),
        "type_gain": bell_draw(key_list[5], (NT, NI), 1.0, 4.0, (), jnp.float32),
        "out_vec": bell_draw(key_list[6], (NT, NO), (NO // 8) ** -0.5, 1.5, (), jnp.float32),
        "targets": bell_draw(key_list[7], (M,), 1.0, 5.0, (), jnp.float32),
        "noise": jnp.clip(jnp.exp(jax.random.uniform(key_list[8], (M,), jnp.float32, math.log(0.05), math.log(2.0))), 0.05, 2.0),
        "cov": draw_cov(jax.random.fold_in(key_list[10], 71), 0),
    }


def reference(atom_feat, types, neighbors, frame_of_atom, weights, type_gain, out_vec, targets, noise, cov):
    hi = lax.Precision.HIGHEST
    groups = N_ROW * N_COL
    frames = ATOM_DEV // FR
    feat = atom_feat.reshape(groups, ATOM_DEV, NI)
    scaled = feat * type_gain[types].reshape(groups, ATOM_DEV, NI)
    nbrs = neighbors.reshape(groups, ATOM_DEV, NB)
    near = jax.vmap(lambda block, index: block[index])(scaled, nbrs)
    desc = jnp.tanh(feat + jnp.mean(near, axis=2))
    act = jnp.tanh(jnp.einsum('gai,ij->gaj', desc, weights, precision=hi))
    row_out = out_vec[types].reshape(groups, ATOM_DEV, NO)
    site_energy = jnp.sum(act * row_out, axis=2)
    slope = (1.0 - act * act) * row_out
    member = (frame_of_atom.reshape(groups, ATOM_DEV)[:, :, None] == jnp.arange(frames)[None, None, :]).astype(jnp.float32)
    pred = (jnp.einsum('ga,gaf->gf', site_energy, member, precision=hi) / FR).reshape(M)
    grad = (jnp.einsum('gaf,gai,gaj->gfij', member, desc, slope, precision=hi) / FR).reshape(M, NW)
    gain_rows = jnp.einsum('ik,mk->im', cov, grad, precision=hi)
    gram = jnp.einsum('mk,kn->mn', grad, gain_rows, precision=hi) + jnp.diag(noise)
    lower = jnp.linalg.cholesky(gram)
    white = jax.scipy.linalg.solve_triangular(lower, gain_rows.T, lower=True)
    coef = jax.scipy.linalg.cho_solve((lower, True), targets - pred)
    new_weights = weights.reshape(-1) + jnp.dot(gain_rows, coef, precision=hi)
    new_cov = cov - jnp.einsum('mi,mj->ij', white, white, precision=hi)
    return (new_weights, new_cov)
```

```python
import jax
import jax.numpy as jnp
from jax import lax
from jax.sharding import PartitionSpec as P

FR = 64


def on_device(
    atom_feat, types, neighbors, frame_of_atom, weights, type_gain, out_vec, targets, noise, cov
):
    hi = lax.Precision.HIGHEST
    mid = lax.Precision.HIGH
    atoms = atom_feat.shape[0]
    ntypes = type_gain.shape[0]
    nbrs = neighbors.shape[1]
    frames = atoms // FR
    onehot_type = (types[:, None] == jnp.arange(ntypes)[None, :]).astype(jnp.float32)
    row_gain = jnp.dot(onehot_type, type_gain, precision=hi)
    row_out = jnp.dot(onehot_type, out_vec, precision=hi)
    scaled = atom_feat * row_gain
    counts = jnp.sum(
        (neighbors[:, :, None] == jnp.arange(atoms)[None, None, :]).astype(jnp.float32), axis=1
    )
    near_sum = jnp.dot(counts, scaled, precision=hi)
    desc = jnp.tanh(atom_feat + near_sum / nbrs)
    act = jnp.tanh(jnp.dot(desc, weights, precision=hi))
    site_energy = jnp.sum(act * row_out, axis=1)
    slope = (1.0 - act * act) * row_out
    member = (frame_of_atom[:, None] == jnp.arange(frames)[None, :]).astype(jnp.float32)
    pred_local = jnp.dot(site_energy, member, precision=hi) / FR
    grads = jnp.einsum("af,ai,aj->fij", member, desc, slope, precision=hi) / FR
    width = grads.shape[1] * grads.shape[2]
    grads = grads.reshape(frames, width)
    n_row = lax.axis_size("row")
    n_col = lax.axis_size("col")
    row_id = lax.axis_index("row")
    col_id = lax.axis_index("col")
    m_all = frames * n_row * n_col
    col_w = width // n_col
    blk = width // (n_row * n_col)
    col_part = lax.all_to_all(grads, "col", split_axis=1, concat_axis=0, tiled=True)
    grad_col = lax.all_gather(col_part, "row", axis=0, tiled=True)
    grad_own = lax.all_to_all(grads, ("row", "col"), split_axis=1, concat_axis=0, tiled=True)
    partial_rows = jnp.einsum("ik,mk->im", cov, grad_col, precision=mid)
    gain_own = lax.psum_scatter(partial_rows, "col", scatter_dimension=0, tiled=True)
    gram_own = jnp.einsum("mk,kn->mn", grad_own, gain_own, precision=hi)
    pred_pad = jnp.zeros((8, m_all), jnp.float32).at[0, :frames].set(pred_local)
    payload = jnp.concatenate([gain_own, gram_own, pred_pad], axis=0)
    gathered = lax.all_gather(payload, "col", axis=0)
    gain_rows = gathered[:, :blk, :].reshape(n_col * blk, m_all)
    gram_row = jnp.sum(gathered[:, blk : blk + m_all, :], axis=0)
    pred_row = gathered[:, blk + m_all, :frames].reshape(n_col * frames)
    slots = lax.dynamic_update_slice_in_dim(
        jnp.zeros((8, m_all), jnp.float32),
        jnp.zeros((8, n_col * frames), jnp.float32).at[0].set(pred_row),
        row_id * n_col * frames,
        1,
    )
    small = lax.psum(jnp.concatenate([gram_row, slots], axis=0), "row")
    gram = small[:m_all] + jnp.diag(noise)
    pred_all = small[m_all]
    lower = jnp.linalg.cholesky(gram)
    factor = n_col // n_row
    half_rows = lax.dynamic_slice_in_dim(gain_rows, col_id % factor * col_w, col_w, 0)
    mine = row_id == col_id // factor
    gain_col = lax.psum(jnp.where(mine, half_rows, jnp.zeros_like(half_rows)), "row")
    white_row = jax.scipy.linalg.solve_triangular(lower, gain_rows.T, lower=True)
    white_col = jax.scipy.linalg.solve_triangular(lower, gain_col.T, lower=True)
    new_cov = cov - jnp.einsum("mi,mj->ij", white_row, white_col, precision=mid)
    coef = jax.scipy.linalg.cho_solve((lower, True), targets - pred_all)
    device_id = row_id * n_col + col_id
    own_weights = lax.dynamic_slice_in_dim(weights.reshape(-1), device_id * blk, blk, 0)
    new_weights = own_weights + jnp.dot(gain_own, coef, precision=hi)
    return (new_weights, new_cov)


def solution(mesh):
    return jax.shard_map(
        on_device,
        mesh=mesh,
        in_specs=(
            P(("row", "col"), None),
            P(("row", "col")),
            P(("row", "col"), None),
            P(("row", "col")),
            P(),
            P(),
            P(),
            P(),
            P(),
            P("row", "col"),
        ),
        out_specs=(P(("row", "col")), P("row", "col")),
        check_vma=False,
    )
```

```python
import jax
import jax.numpy as jnp
from jax import lax
from jax.sharding import PartitionSpec as P

FR = 64


def broadcast_rows(buf, n_row, n_col, factor):
    bits = []
    b = 1
    while b < n_row:
        bits.append(b)
        b *= 2
    bits = bits[1:][::-1] + bits[:1]
    held = [0]
    for bit in bits:
        perm = []
        for c in range(n_col):
            s = c // factor
            for rel in held:
                perm.append(((s ^ rel) * n_col + c, (s ^ rel ^ bit) * n_col + c))
        buf = buf + lax.ppermute(buf, ("row", "col"), perm)
        held = held + [rel ^ bit for rel in held]
    return buf


def on_device(
    atom_feat, types, neighbors, frame_of_atom, weights, type_gain, out_vec, targets, noise, cov
):
    hi = lax.Precision.HIGHEST
    mid = lax.Precision.HIGH
    atoms = atom_feat.shape[0]
    ntypes = type_gain.shape[0]
    nbrs = neighbors.shape[1]
    frames = atoms // FR
    onehot_type = (types[:, None] == jnp.arange(ntypes)[None, :]).astype(jnp.float32)
    row_gain = jnp.dot(onehot_type, type_gain, precision=hi)
    row_out = jnp.dot(onehot_type, out_vec, precision=hi)
    scaled = atom_feat * row_gain
    counts = jnp.sum(
        (neighbors[:, :, None] == jnp.arange(atoms)[None, None, :]).astype(jnp.float32), axis=1
    )
    near_sum = jnp.dot(counts, scaled, precision=hi)
    desc = jnp.tanh(atom_feat + near_sum / nbrs)
    act = jnp.tanh(jnp.dot(desc, weights, precision=hi))
    site_energy = jnp.sum(act * row_out, axis=1)
    slope = (1.0 - act * act) * row_out
    member = (frame_of_atom[:, None] == jnp.arange(frames)[None, :]).astype(jnp.float32)
    pred_local = jnp.dot(site_energy, member, precision=hi) / FR
    grads = jnp.einsum("af,ai,aj->fij", member, desc, slope, precision=hi) / FR
    width = grads.shape[1] * grads.shape[2]
    grads = grads.reshape(frames, width)
    n_row = lax.axis_size("row")
    n_col = lax.axis_size("col")
    row_id = lax.axis_index("row")
    col_id = lax.axis_index("col")
    m_all = frames * n_row * n_col
    col_w = width // n_col
    blk = width // (n_row * n_col)
    col_part = lax.all_to_all(grads, "col", split_axis=1, concat_axis=0, tiled=True)
    grad_col = lax.all_gather(col_part, "row", axis=0, tiled=True)
    grad_own = lax.all_to_all(grads, ("row", "col"), split_axis=1, concat_axis=0, tiled=True)
    partial_rows = jnp.einsum("ik,mk->im", cov, grad_col, precision=mid)
    gain_own = lax.psum_scatter(partial_rows, "col", scatter_dimension=0, tiled=True)
    gram_own = jnp.einsum("mk,kn->mn", grad_own, gain_own, precision=hi)
    pred_pad = jnp.zeros((8, m_all), jnp.float32).at[0, :frames].set(pred_local)
    payload = jnp.concatenate([gain_own, gram_own, pred_pad], axis=0)
    gathered = lax.all_gather(payload, "col", axis=0)
    gain_rows = gathered[:, :blk, :].reshape(n_col * blk, m_all)
    gram_row = jnp.sum(gathered[:, blk : blk + m_all, :], axis=0)
    pred_row = gathered[:, blk + m_all, :frames].reshape(n_col * frames)
    slots = lax.dynamic_update_slice_in_dim(
        jnp.zeros((8, m_all), jnp.float32),
        jnp.zeros((8, n_col * frames), jnp.float32).at[0].set(pred_row),
        row_id * n_col * frames,
        1,
    )
    small = lax.psum(jnp.concatenate([gram_row, slots], axis=0), "row")
    gram = small[:m_all] + jnp.diag(noise)
    pred_all = small[m_all]
    lower = jnp.linalg.cholesky(gram)
    factor = n_col // n_row
    half_rows = lax.dynamic_slice_in_dim(gain_rows, col_id % factor * col_w, col_w, 0)
    mine = row_id == col_id // factor
    gain_col = broadcast_rows(jnp.where(mine, half_rows, jnp.zeros_like(half_rows)), n_row, n_col, factor)
    white_row = jax.scipy.linalg.solve_triangular(lower, gain_rows.T, lower=True)
    white_col = jax.scipy.linalg.solve_triangular(lower, gain_col.T, lower=True)
    new_cov = cov - jnp.einsum("mi,mj->ij", white_row, white_col, precision=mid)
    coef = jax.scipy.linalg.cho_solve((lower, True), targets - pred_all)
    device_id = row_id * n_col + col_id
    own_weights = lax.dynamic_slice_in_dim(weights.reshape(-1), device_id * blk, blk, 0)
    new_weights = own_weights + jnp.dot(gain_own, coef, precision=hi)
    return (new_weights, new_cov)


def solution(mesh):
    return jax.shard_map(
        on_device,
        mesh=mesh,
        in_specs=(
            P(("row", "col"), None),
            P(("row", "col")),
            P(("row", "col"), None),
            P(("row", "col")),
            P(),
            P(),
            P(),
            P(),
            P(),
            P("row", "col"),
        ),
        out_specs=(P(("row", "col")), P("row", "col")),
        check_vma=False,
    )
```

```python
import jax
import jax.numpy as jnp
from jax import lax
from jax.sharding import PartitionSpec as P

FR = 64


def broadcast_rows(buf, n_row, n_col, factor):
    bits = []
    b = 1
    while b < n_row:
        bits.append(b)
        b *= 2
    bits = bits[1:][::-1] + bits[:1]
    held = [0]
    for bit in bits:
        perm = []
        for c in range(n_col):
            s = c // factor
            for rel in held:
                perm.append(((s ^ rel) * n_col + c, (s ^ rel ^ bit) * n_col + c))
        buf = buf + lax.ppermute(buf, ("row", "col"), perm)
        held = held + [rel ^ bit for rel in held]
    return buf


def butterfly_sum(buf, axis, size):
    bit = 1
    while bit < size:
        buf = buf + lax.ppermute(buf, axis, [(i, i ^ bit) for i in range(size)])
        bit *= 2
    return buf


def on_device(
    atom_feat, types, neighbors, frame_of_atom, weights, type_gain, out_vec, targets, noise, cov
):
    hi = lax.Precision.HIGHEST
    mid = lax.Precision.HIGH
    atoms = atom_feat.shape[0]
    ntypes = type_gain.shape[0]
    nbrs = neighbors.shape[1]
    frames = atoms // FR
    onehot_type = (types[:, None] == jnp.arange(ntypes)[None, :]).astype(jnp.float32)
    row_gain = jnp.dot(onehot_type, type_gain, precision=hi)
    row_out = jnp.dot(onehot_type, out_vec, precision=hi)
    scaled = atom_feat * row_gain
    counts = jnp.sum(
        (neighbors[:, :, None] == jnp.arange(atoms)[None, None, :]).astype(jnp.float32), axis=1
    )
    near_sum = jnp.dot(counts, scaled, precision=hi)
    desc = jnp.tanh(atom_feat + near_sum / nbrs)
    act = jnp.tanh(jnp.dot(desc, weights, precision=hi))
    site_energy = jnp.sum(act * row_out, axis=1)
    slope = (1.0 - act * act) * row_out
    member = (frame_of_atom[:, None] == jnp.arange(frames)[None, :]).astype(jnp.float32)
    pred_local = jnp.dot(site_energy, member, precision=hi) / FR
    grads = jnp.einsum("af,ai,aj->fij", member, desc, slope, precision=hi) / FR
    width = grads.shape[1] * grads.shape[2]
    grads = grads.reshape(frames, width)
    n_row = lax.axis_size("row")
    n_col = lax.axis_size("col")
    row_id = lax.axis_index("row")
    col_id = lax.axis_index("col")
    m_all = frames * n_row * n_col
    col_w = width // n_col
    blk = width // (n_row * n_col)
    col_part = lax.all_to_all(grads, "col", split_axis=1, concat_axis=0, tiled=True)
    grad_col = lax.all_gather(col_part, "row", axis=0, tiled=True)
    grad_own = lax.all_to_all(grads, ("row", "col"), split_axis=1, concat_axis=0, tiled=True)
    partial_rows = jnp.einsum("ik,mk->im", cov, grad_col, precision=mid)
    gain_own = lax.psum_scatter(partial_rows, "col", scatter_dimension=0, tiled=True)
    gram_own = jnp.einsum("mk,kn->mn", grad_own, gain_own, precision=hi)
    pred_pad = jnp.zeros((8, m_all), jnp.float32).at[0, :frames].set(pred_local)
    payload = jnp.concatenate([gain_own, gram_own, pred_pad], axis=0)
    gathered = lax.all_gather(payload, "col", axis=0)
    gain_rows = gathered[:, :blk, :].reshape(n_col * blk, m_all)
    gram_row = jnp.sum(gathered[:, blk : blk + m_all, :], axis=0)
    pred_row = gathered[:, blk + m_all, :frames].reshape(n_col * frames)
    slots = lax.dynamic_update_slice_in_dim(
        jnp.zeros((8, m_all), jnp.float32),
        jnp.zeros((8, n_col * frames), jnp.float32).at[0].set(pred_row),
        row_id * n_col * frames,
        1,
    )
    small = butterfly_sum(jnp.concatenate([gram_row, slots], axis=0), "row", n_row)
    gram = small[:m_all] + jnp.diag(noise)
    pred_all = small[m_all]
    lower = jnp.linalg.cholesky(gram)
    factor = n_col // n_row
    half_rows = lax.dynamic_slice_in_dim(gain_rows, col_id % factor * col_w, col_w, 0)
    mine = row_id == col_id // factor
    gain_col = broadcast_rows(jnp.where(mine, half_rows, jnp.zeros_like(half_rows)), n_row, n_col, factor)
    white_row = jax.scipy.linalg.solve_triangular(lower, gain_rows.T, lower=True)
    white_col = jax.scipy.linalg.solve_triangular(lower, gain_col.T, lower=True)
    new_cov = cov - jnp.einsum("mi,mj->ij", white_row, white_col, precision=mid)
    coef = jax.scipy.linalg.cho_solve((lower, True), targets - pred_all)
    device_id = row_id * n_col + col_id
    own_weights = lax.dynamic_slice_in_dim(weights.reshape(-1), device_id * blk, blk, 0)
    new_weights = own_weights + jnp.dot(gain_own, coef, precision=hi)
    return (new_weights, new_cov)


def solution(mesh):
    return jax.shard_map(
        on_device,
        mesh=mesh,
        in_specs=(
            P(("row", "col"), None),
            P(("row", "col")),
            P(("row", "col"), None),
            P(("row", "col")),
            P(),
            P(),
            P(),
            P(),
            P(),
            P("row", "col"),
        ),
        out_specs=(P(("row", "col")), P("row", "col")),
        check_vma=False,
    )
```

```python
import jax
import jax.numpy as jnp
from jax import lax
from jax.sharding import PartitionSpec as P

FR = 64


def broadcast_rows(buf, n_row, n_col, factor):
    bits = []
    b = 1
    while b < n_row:
        bits.append(b)
        b *= 2
    bits = bits[1:][::-1] + bits[:1]
    held = [0]
    for bit in bits:
        perm = []
        for c in range(n_col):
            s = c // factor
            for rel in held:
                perm.append(((s ^ rel) * n_col + c, (s ^ rel ^ bit) * n_col + c))
        buf = buf + lax.ppermute(buf, ("row", "col"), perm)
        held = held + [rel ^ bit for rel in held]
    return buf


def butterfly_sum(buf, axis, size):
    bit = 1
    while bit < size:
        buf = buf + lax.ppermute(buf, axis, [(i, i ^ bit) for i in range(size)])
        bit *= 2
    return buf


def halving_scatter(x, axis, size, me):
    nbits = size.bit_length() - 1
    x = x.reshape((2,) * nbits + (x.shape[0] // size,) + x.shape[1:])
    for step in range(nbits):
        bit = 1 << step
        dim = nbits - 1 - step
        mine = (me // bit) % 2
        keep = lax.dynamic_index_in_dim(x, mine, dim, keepdims=False)
        send = lax.dynamic_index_in_dim(x, 1 - mine, dim, keepdims=False)
        x = keep + lax.ppermute(send, axis, [(i, i ^ bit) for i in range(size)])
    return x


def on_device(
    atom_feat, types, neighbors, frame_of_atom, weights, type_gain, out_vec, targets, noise, cov
):
    hi = lax.Precision.HIGHEST
    mid = lax.Precision.HIGH
    atoms = atom_feat.shape[0]
    ntypes = type_gain.shape[0]
    nbrs = neighbors.shape[1]
    frames = atoms // FR
    onehot_type = (types[:, None] == jnp.arange(ntypes)[None, :]).astype(jnp.float32)
    row_gain = jnp.dot(onehot_type, type_gain, precision=hi)
    row_out = jnp.dot(onehot_type, out_vec, precision=hi)
    scaled = atom_feat * row_gain
    counts = jnp.sum(
        (neighbors[:, :, None] == jnp.arange(atoms)[None, None, :]).astype(jnp.float32), axis=1
    )
    near_sum = jnp.dot(counts, scaled, precision=hi)
    desc = jnp.tanh(atom_feat + near_sum / nbrs)
    act = jnp.tanh(jnp.dot(desc, weights, precision=hi))
    site_energy = jnp.sum(act * row_out, axis=1)
    slope = (1.0 - act * act) * row_out
    member = (frame_of_atom[:, None] == jnp.arange(frames)[None, :]).astype(jnp.float32)
    pred_local = jnp.dot(site_energy, member, precision=hi) / FR
    grads = jnp.einsum("af,ai,aj->fij", member, desc, slope, precision=hi) / FR
    width = grads.shape[1] * grads.shape[2]
    grads = grads.reshape(frames, width)
    n_row = lax.axis_size("row")
    n_col = lax.axis_size("col")
    row_id = lax.axis_index("row")
    col_id = lax.axis_index("col")
    m_all = frames * n_row * n_col
    col_w = width // n_col
    blk = width // (n_row * n_col)
    col_part = lax.all_to_all(grads, "col", split_axis=1, concat_axis=0, tiled=True)
    grad_col = lax.all_gather(col_part, "row", axis=0, tiled=True)
    grad_own = lax.all_to_all(grads, ("row", "col"), split_axis=1, concat_axis=0, tiled=True)
    partial_rows = jnp.einsum("ik,mk->im", cov, grad_col, precision=mid)
    gain_own = halving_scatter(partial_rows, "col", n_col, col_id)
    gram_own = jnp.einsum("mk,kn->mn", grad_own, gain_own, precision=hi)
    pred_pad = jnp.zeros((8, m_all), jnp.float32).at[0, :frames].set(pred_local)
    payload = jnp.concatenate([gain_own, gram_own, pred_pad], axis=0)
    gathered = lax.all_gather(payload, "col", axis=0)
    gain_rows = gathered[:, :blk, :].reshape(n_col * blk, m_all)
    gram_row = jnp.sum(gathered[:, blk : blk + m_all, :], axis=0)
    pred_row = gathered[:, blk + m_all, :frames].reshape(n_col * frames)
    slots = lax.dynamic_update_slice_in_dim(
        jnp.zeros((8, m_all), jnp.float32),
        jnp.zeros((8, n_col * frames), jnp.float32).at[0].set(pred_row),
        row_id * n_col * frames,
        1,
    )
    small = butterfly_sum(jnp.concatenate([gram_row, slots], axis=0), "row", n_row)
    gram = small[:m_all] + jnp.diag(noise)
    pred_all = small[m_all]
    lower = jnp.linalg.cholesky(gram)
    factor = n_col // n_row
    half_rows = lax.dynamic_slice_in_dim(gain_rows, col_id % factor * col_w, col_w, 0)
    mine = row_id == col_id // factor
    gain_col = broadcast_rows(jnp.where(mine, half_rows, jnp.zeros_like(half_rows)), n_row, n_col, factor)
    white_row = jax.scipy.linalg.solve_triangular(lower, gain_rows.T, lower=True)
    white_col = jax.scipy.linalg.solve_triangular(lower, gain_col.T, lower=True)
    new_cov = cov - jnp.einsum("mi,mj->ij", white_row, white_col, precision=mid)
    coef = jax.scipy.linalg.cho_solve((lower, True), targets - pred_all)
    device_id = row_id * n_col + col_id
    own_weights = lax.dynamic_slice_in_dim(weights.reshape(-1), device_id * blk, blk, 0)
    new_weights = own_weights + jnp.dot(gain_own, coef, precision=hi)
    return (new_weights, new_cov)


def solution(mesh):
    return jax.shard_map(
        on_device,
        mesh=mesh,
        in_specs=(
            P(("row", "col"), None),
            P(("row", "col")),
            P(("row", "col"), None),
            P(("row", "col")),
            P(),
            P(),
            P(),
            P(),
            P(),
            P("row", "col"),
        ),
        out_specs=(P(("row", "col")), P("row", "col")),
        check_vma=False,
    )
```

```python
import jax
import jax.numpy as jnp
from jax import lax
from jax.sharding import PartitionSpec as P

FR = 64


def broadcast_rows(buf, n_row, n_col, factor):
    bits = []
    b = 1
    while b < n_row:
        bits.append(b)
        b *= 2
    bits = bits[1:][::-1] + bits[:1]
    held = [0]
    for bit in bits:
        perm = []
        for c in range(n_col):
            s = c // factor
            for rel in held:
                perm.append(((s ^ rel) * n_col + c, (s ^ rel ^ bit) * n_col + c))
        buf = buf + lax.ppermute(buf, ("row", "col"), perm)
        held = held + [rel ^ bit for rel in held]
    return buf


def butterfly_sum(buf, axis, size):
    bit = 1
    while bit < size:
        buf = buf + lax.ppermute(buf, axis, [(i, i ^ bit) for i in range(size)])
        bit *= 2
    return buf


def halving_scatter(x, axis, size, me):
    nbits = size.bit_length() - 1
    x = x.reshape((2,) * nbits + (x.shape[0] // size,) + x.shape[1:])
    for step in range(nbits):
        bit = 1 << step
        dim = nbits - 1 - step
        mine = (me // bit) % 2
        keep = lax.dynamic_index_in_dim(x, mine, dim, keepdims=False)
        send = lax.dynamic_index_in_dim(x, 1 - mine, dim, keepdims=False)
        x = keep + lax.ppermute(send, axis, [(i, i ^ bit) for i in range(size)])
    return x


def on_device(
    atom_feat, types, neighbors, frame_of_atom, weights, type_gain, out_vec, targets, noise, cov
):
    hi = lax.Precision.HIGHEST
    mid = lax.Precision.HIGH
    atoms = atom_feat.shape[0]
    ntypes = type_gain.shape[0]
    nbrs = neighbors.shape[1]
    frames = atoms // FR
    onehot_type = (types[:, None] == jnp.arange(ntypes)[None, :]).astype(jnp.float32)
    row_gain = jnp.dot(onehot_type, type_gain, precision=hi)
    row_out = jnp.dot(onehot_type, out_vec, precision=hi)
    scaled = atom_feat * row_gain
    counts = jnp.sum(
        (neighbors[:, :, None] == jnp.arange(atoms)[None, None, :]).astype(jnp.float32), axis=1
    )
    near_sum = jnp.dot(counts, scaled, precision=hi)
    desc = jnp.tanh(atom_feat + near_sum / nbrs)
    act = jnp.tanh(jnp.dot(desc, weights, precision=hi))
    site_energy = jnp.sum(act * row_out, axis=1)
    slope = (1.0 - act * act) * row_out
    member = (frame_of_atom[:, None] == jnp.arange(frames)[None, :]).astype(jnp.float32)
    pred_local = jnp.dot(site_energy, member, precision=hi) / FR
    grads = jnp.einsum("af,ai,aj->fij", member, desc, slope, precision=hi) / FR
    width = grads.shape[1] * grads.shape[2]
    grads = grads.reshape(frames, width)
    n_row = lax.axis_size("row")
    n_col = lax.axis_size("col")
    row_id = lax.axis_index("row")
    col_id = lax.axis_index("col")
    m_all = frames * n_row * n_col
    col_w = width // n_col
    blk = width // (n_row * n_col)
    col_part = lax.all_to_all(grads, "col", split_axis=1, concat_axis=0, tiled=True)
    grad_col = lax.all_gather(col_part, "row", axis=0, tiled=True)
    grad_own = lax.all_to_all(grads, ("row", "col"), split_axis=1, concat_axis=0, tiled=True)
    partial_rows = jnp.einsum("ik,mk->im", cov, grad_col, precision=mid)
    gain_own = halving_scatter(partial_rows, "col", n_col, col_id)
    gram_own = jnp.einsum("mk,kn->mn", grad_own, gain_own, precision=hi)
    device_id = row_id * n_col + col_id
    slots = lax.dynamic_update_slice_in_dim(
        jnp.zeros((8, m_all), jnp.float32),
        jnp.zeros((8, frames), jnp.float32).at[0].set(pred_local),
        device_id * frames,
        1,
    )
    small = jnp.concatenate([gram_own, slots], axis=0)
    small = butterfly_sum(butterfly_sum(small, "col", n_col), "row", n_row)
    gram = small[:m_all] + jnp.diag(noise)
    pred_all = small[m_all]
    gain_rows = lax.all_gather(gain_own, "col", axis=0, tiled=True)
    lower = jnp.linalg.cholesky(gram)
    factor = n_col // n_row
    half_rows = lax.dynamic_slice_in_dim(gain_rows, col_id % factor * col_w, col_w, 0)
    mine = row_id == col_id // factor
    gain_col = broadcast_rows(jnp.where(mine, half_rows, jnp.zeros_like(half_rows)), n_row, n_col, factor)
    white_row = jax.scipy.linalg.solve_triangular(lower, gain_rows.T, lower=True)
    white_col = jax.scipy.linalg.solve_triangular(lower, gain_col.T, lower=True)
    new_cov = cov - jnp.einsum("mi,mj->ij", white_row, white_col, precision=mid)
    coef = jax.scipy.linalg.cho_solve((lower, True), targets - pred_all)
    own_weights = lax.dynamic_slice_in_dim(weights.reshape(-1), device_id * blk, blk, 0)
    new_weights = own_weights + jnp.dot(gain_own, coef, precision=hi)
    return (new_weights, new_cov)


def solution(mesh):
    return jax.shard_map(
        on_device,
        mesh=mesh,
        in_specs=(
            P(("row", "col"), None),
            P(("row", "col")),
            P(("row", "col"), None),
            P(("row", "col")),
            P(),
            P(),
            P(),
            P(),
            P(),
            P("row", "col"),
        ),
        out_specs=(P(("row", "col")), P("row", "col")),
        check_vma=False,
    )
```

```python
import jax
import jax.numpy as jnp
from jax import lax
from jax.sharding import PartitionSpec as P

FR = 64


def broadcast_rows(buf, n_row, n_col, factor):
    bits = []
    b = 1
    while b < n_row:
        bits.append(b)
        b *= 2
    bits = bits[1:][::-1] + bits[:1]
    held = [0]
    for bit in bits:
        perm = []
        for c in range(n_col):
            s = c // factor
            for rel in held:
                perm.append(((s ^ rel) * n_col + c, (s ^ rel ^ bit) * n_col + c))
        buf = buf + lax.ppermute(buf, ("row", "col"), perm)
        held = held + [rel ^ bit for rel in held]
    return buf


def butterfly_sum(buf, axis, size):
    bit = 1
    while bit < size:
        buf = buf + lax.ppermute(buf, axis, [(i, i ^ bit) for i in range(size)])
        bit *= 2
    return buf


def halving_scatter(x, axis, size, me):
    nbits = size.bit_length() - 1
    for step in range(nbits):
        bit = 1 << step
        mine = (me // bit) % 2
        keep = lax.dynamic_index_in_dim(x, mine, 0, keepdims=False)
        send = lax.dynamic_index_in_dim(x, 1 - mine, 0, keepdims=False)
        x = keep + lax.ppermute(send, axis, [(i, i ^ bit) for i in range(size)])
    return x


def on_device(
    atom_feat, types, neighbors, frame_of_atom, weights, type_gain, out_vec, targets, noise, cov
):
    hi = lax.Precision.HIGHEST
    mid = lax.Precision.HIGH
    atoms = atom_feat.shape[0]
    ntypes = type_gain.shape[0]
    nbrs = neighbors.shape[1]
    frames = atoms // FR
    onehot_type = (types[:, None] == jnp.arange(ntypes)[None, :]).astype(jnp.float32)
    row_gain = jnp.dot(onehot_type, type_gain, precision=hi)
    row_out = jnp.dot(onehot_type, out_vec, precision=hi)
    scaled = atom_feat * row_gain
    counts = jnp.sum(
        (neighbors[:, :, None] == jnp.arange(atoms)[None, None, :]).astype(jnp.float32), axis=1
    )
    near_sum = jnp.dot(counts, scaled, precision=hi)
    desc = jnp.tanh(atom_feat + near_sum / nbrs)
    act = jnp.tanh(jnp.dot(desc, weights, precision=hi))
    site_energy = jnp.sum(act * row_out, axis=1)
    slope = (1.0 - act * act) * row_out
    member = (frame_of_atom[:, None] == jnp.arange(frames)[None, :]).astype(jnp.float32)
    pred_local = jnp.dot(site_energy, member, precision=hi) / FR
    grads = jnp.einsum("af,ai,aj->fij", member, desc, slope, precision=hi) / FR
    width = grads.shape[1] * grads.shape[2]
    grads = grads.reshape(frames, width)
    n_row = lax.axis_size("row")
    n_col = lax.axis_size("col")
    row_id = lax.axis_index("row")
    col_id = lax.axis_index("col")
    m_all = frames * n_row * n_col
    col_w = width // n_col
    blk = width // (n_row * n_col)
    col_part = lax.all_to_all(grads, "col", split_axis=1, concat_axis=0, tiled=True)
    grad_col = lax.all_gather(col_part, "row", axis=0, tiled=True)
    grad_own = lax.all_to_all(grads, ("row", "col"), split_axis=1, concat_axis=0, tiled=True)
    grad_own, grad_col = lax.optimization_barrier((grad_own, grad_col))
    nbits = n_col.bit_length() - 1
    letters = "abcdefgh"[:nbits]
    cov_blocks = cov.reshape((2,) * nbits + (cov.shape[0] // n_col, cov.shape[1]))
    partial_t = jnp.einsum(
        "mk," + letters + "ik->" + letters[::-1] + "mi", grad_col, cov_blocks, precision=mid
    )
    gain_own_t = halving_scatter(partial_t, "col", n_col, col_id)
    gram_own = jnp.einsum("mk,nk->mn", grad_own, gain_own_t, precision=hi)
    device_id = row_id * n_col + col_id
    slots = lax.dynamic_update_slice_in_dim(
        jnp.zeros((8, m_all), jnp.float32),
        jnp.zeros((8, frames), jnp.float32).at[0].set(pred_local),
        device_id * frames,
        1,
    )
    small = jnp.concatenate([gram_own, slots], axis=0)
    small = butterfly_sum(butterfly_sum(small, "col", n_col), "row", n_row)
    gram = small[:m_all] + jnp.diag(noise)
    pred_all = small[m_all]
    gain_rows_t = lax.all_gather(gain_own_t, "col", axis=1, tiled=True)
    lower = jnp.linalg.cholesky(gram)
    factor = n_col // n_row
    half_t = lax.dynamic_slice_in_dim(gain_rows_t, col_id % factor * col_w, col_w, 1)
    mine = row_id == col_id // factor
    gain_col_t = broadcast_rows(jnp.where(mine, half_t, jnp.zeros_like(half_t)), n_row, n_col, factor)
    white_row = jax.scipy.linalg.solve_triangular(lower, gain_rows_t, lower=True)
    white_col = jax.scipy.linalg.solve_triangular(lower, gain_col_t, lower=True)
    new_cov = cov - jnp.einsum("mi,mj->ij", white_row, white_col, precision=mid)
    coef = jax.scipy.linalg.cho_solve((lower, True), targets - pred_all)
    own_weights = lax.dynamic_slice_in_dim(weights.reshape(-1), device_id * blk, blk, 0)
    new_weights = own_weights + jnp.dot(coef, gain_own_t, precision=hi)
    return (new_weights, new_cov)


def solution(mesh):
    return jax.shard_map(
        on_device,
        mesh=mesh,
        in_specs=(
            P(("row", "col"), None),
            P(("row", "col")),
            P(("row", "col"), None),
            P(("row", "col")),
            P(),
            P(),
            P(),
            P(),
            P(),
            P("row", "col"),
        ),
        out_specs=(P(("row", "col")), P("row", "col")),
        check_vma=False,
    )
```

```python
import jax
import jax.numpy as jnp
from jax import lax
from jax.sharding import PartitionSpec as P

FR = 64


def broadcast_rows(buf, n_row, n_col, factor):
    bits = []
    b = 1
    while b < n_row:
        bits.append(b)
        b *= 2
    bits = bits[1:][::-1] + bits[:1]
    held = [0]
    for bit in bits:
        perm = []
        for c in range(n_col):
            s = c // factor
            for rel in held:
                perm.append(((s ^ rel) * n_col + c, (s ^ rel ^ bit) * n_col + c))
        buf = buf + lax.ppermute(buf, ("row", "col"), perm)
        held = held + [rel ^ bit for rel in held]
    return buf


def butterfly_sum(buf, axis, size):
    bit = 1
    while bit < size:
        buf = buf + lax.ppermute(buf, axis, [(i, i ^ bit) for i in range(size)])
        bit *= 2
    return buf


def halving_scatter(x, axis, size, me):
    nbits = size.bit_length() - 1
    for step in range(nbits):
        bit = 1 << step
        mine = (me // bit) % 2
        keep = lax.dynamic_index_in_dim(x, mine, 0, keepdims=False)
        send = lax.dynamic_index_in_dim(x, 1 - mine, 0, keepdims=False)
        x = keep + lax.ppermute(send, axis, [(i, i ^ bit) for i in range(size)])
    return x


def on_device(
    atom_feat, types, neighbors, frame_of_atom, weights, type_gain, out_vec, targets, noise, cov
):
    hi = lax.Precision.HIGHEST
    mid = lax.Precision.HIGH
    atoms = atom_feat.shape[0]
    ntypes = type_gain.shape[0]
    nbrs = neighbors.shape[1]
    frames = atoms // FR
    onehot_type = (types[:, None] == jnp.arange(ntypes)[None, :]).astype(jnp.float32)
    row_gain = jnp.dot(onehot_type, type_gain, precision=hi)
    row_out = jnp.dot(onehot_type, out_vec, precision=hi)
    scaled = atom_feat * row_gain
    counts = jnp.sum(
        (neighbors[:, :, None] == jnp.arange(atoms)[None, None, :]).astype(jnp.float32), axis=1
    )
    near_sum = jnp.dot(counts, scaled, precision=hi)
    desc = jnp.tanh(atom_feat + near_sum / nbrs)
    act = jnp.tanh(jnp.dot(desc, weights, precision=hi))
    site_energy = jnp.sum(act * row_out, axis=1)
    slope = (1.0 - act * act) * row_out
    member = (frame_of_atom[:, None] == jnp.arange(frames)[None, :]).astype(jnp.float32)
    pred_local = jnp.dot(site_energy, member, precision=hi) / FR
    grads = jnp.einsum("af,ai,aj->fij", member, desc, slope, precision=hi) / FR
    width = grads.shape[1] * grads.shape[2]
    grads = grads.reshape(frames, width)
    n_row = lax.axis_size("row")
    n_col = lax.axis_size("col")
    row_id = lax.axis_index("row")
    col_id = lax.axis_index("col")
    m_all = frames * n_row * n_col
    col_w = width // n_col
    blk = width // (n_row * n_col)
    col_part = lax.all_to_all(grads, "col", split_axis=1, concat_axis=0, tiled=True)
    grad_col = lax.all_gather(col_part, "row", axis=0, tiled=True)
    nbits = n_col.bit_length() - 1
    letters = "abcdefgh"[:nbits]
    cov_blocks = cov.reshape((2,) * nbits + (cov.shape[0] // n_col, cov.shape[1]))
    partial_t = jnp.einsum(
        "mk," + letters + "ik->" + letters[::-1] + "mi", grad_col, cov_blocks, precision=mid
    )
    gain_own_t = halving_scatter(partial_t, "col", n_col, col_id)
    gain_rows_t = lax.all_gather(gain_own_t, "col", axis=1, tiled=True)
    factor = n_col // n_row
    half_t = lax.dynamic_slice_in_dim(gain_rows_t, col_id % factor * col_w, col_w, 1)
    mine = row_id == col_id // factor
    gram_part = jnp.einsum("mk,nk->mn", grad_col, half_t, precision=hi)
    gram_part = jnp.where(mine, gram_part, jnp.zeros_like(gram_part))
    device_id = row_id * n_col + col_id
    slots = lax.dynamic_update_slice_in_dim(
        jnp.zeros((8, m_all), jnp.float32),
        jnp.zeros((8, frames), jnp.float32).at[0].set(pred_local),
        device_id * frames,
        1,
    )
    small = jnp.concatenate([gram_part, slots], axis=0)
    small = butterfly_sum(butterfly_sum(small, "col", n_col), "row", n_row)
    masked = jnp.where(mine, half_t, jnp.zeros_like(half_t))
    small, masked = lax.optimization_barrier((small, masked))
    gram = small[:m_all] + jnp.diag(noise)
    pred_all = small[m_all]
    lower = jnp.linalg.cholesky(gram)
    gain_col_t = broadcast_rows(masked, n_row, n_col, factor)
    white_row = jax.scipy.linalg.solve_triangular(lower, gain_rows_t, lower=True)
    white_col = jax.scipy.linalg.solve_triangular(lower, gain_col_t, lower=True)
    new_cov = cov - jnp.einsum("mi,mj->ij", white_row, white_col, precision=mid)
    coef = jax.scipy.linalg.cho_solve((lower, True), targets - pred_all)
    own_weights = lax.dynamic_slice_in_dim(weights.reshape(-1), device_id * blk, blk, 0)
    new_weights = own_weights + jnp.dot(coef, gain_own_t, precision=hi)
    return (new_weights, new_cov)


def solution(mesh):
    return jax.shard_map(
        on_device,
        mesh=mesh,
        in_specs=(
            P(("row", "col"), None),
            P(("row", "col")),
            P(("row", "col"), None),
            P(("row", "col")),
            P(),
            P(),
            P(),
            P(),
            P(),
            P("row", "col"),
        ),
        out_specs=(P(("row", "col")), P("row", "col")),
        check_vma=False,
    )
```

```python
import jax
import jax.numpy as jnp
from jax import lax
from jax.sharding import PartitionSpec as P

FR = 64


def broadcast_rows(buf, n_row, n_col, factor):
    bits = []
    b = 1
    while b < n_row:
        bits.append(b)
        b *= 2
    bits = bits[1:][::-1] + bits[:1]
    held = [0]
    for bit in bits:
        perm = []
        for c in range(n_col):
            s = c // factor
            for rel in held:
                perm.append(((s ^ rel) * n_col + c, (s ^ rel ^ bit) * n_col + c))
        buf = buf + lax.ppermute(buf, ("row", "col"), perm)
        held = held + [rel ^ bit for rel in held]
    return buf


def butterfly_sum(buf, axis, size):
    bit = 1
    while bit < size:
        buf = buf + lax.ppermute(buf, axis, [(i, i ^ bit) for i in range(size)])
        bit *= 2
    return buf


def halving_scatter(x, axis, size, me):
    nbits = size.bit_length() - 1
    for step in range(nbits):
        bit = 1 << step
        mine = (me // bit) % 2
        keep = lax.dynamic_index_in_dim(x, mine, 0, keepdims=False)
        send = lax.dynamic_index_in_dim(x, 1 - mine, 0, keepdims=False)
        x = keep + lax.ppermute(send, axis, [(i, i ^ bit) for i in range(size)])
    return x


def shift_all_to_all(x, axis, size, me):
    got = [lax.dynamic_index_in_dim(x, me, 1, keepdims=False)]
    for k in range(1, size):
        piece = lax.dynamic_index_in_dim(x, (me + size - k) % size, 1, keepdims=False)
        got.append(lax.ppermute(piece, axis, [(i, (i - k) % size) for i in range(size)]))
    got = jnp.stack(got, axis=0)
    both = jnp.concatenate([got, got], axis=0)
    ordered = lax.dynamic_slice_in_dim(both, (size - me) % size, size, 0)
    return ordered.reshape((size * x.shape[0],) + x.shape[2:])


def doubling_gather(x, axis, size, me):
    bits = []
    bit = 1
    while bit < size:
        bits.append(bit)
        bit *= 2
    rows = x.shape[0]
    x = x[None]
    for bit in bits[::-1]:
        other = lax.ppermute(x, axis, [(i, i ^ bit) for i in range(size)])
        low = (me // bit) % 2 == 0
        x = jnp.where(low, jnp.stack([x, other], axis=1), jnp.stack([other, x], axis=1))
        x = x.reshape((x.shape[0] * 2,) + x.shape[2:])
    return x.reshape((size * rows,) + x.shape[2:])


def on_device(
    atom_feat, types, neighbors, frame_of_atom, weights, type_gain, out_vec, targets, noise, cov
):
    hi = lax.Precision.HIGHEST
    mid = lax.Precision.HIGH
    atoms = atom_feat.shape[0]
    ntypes = type_gain.shape[0]
    nbrs = neighbors.shape[1]
    frames = atoms // FR
    onehot_type = (types[:, None] == jnp.arange(ntypes)[None, :]).astype(jnp.float32)
    row_gain = jnp.dot(onehot_type, type_gain, precision=hi)
    row_out = jnp.dot(onehot_type, out_vec, precision=hi)
    scaled = atom_feat * row_gain
    counts = jnp.sum(
        (neighbors[:, :, None] == jnp.arange(atoms)[None, None, :]).astype(jnp.float32), axis=1
    )
    near_sum = jnp.dot(counts, scaled, precision=hi)
    desc = jnp.tanh(atom_feat + near_sum / nbrs)
    act = jnp.tanh(jnp.dot(desc, weights, precision=hi))
    site_energy = jnp.sum(act * row_out, axis=1)
    slope = (1.0 - act * act) * row_out
    member = (frame_of_atom[:, None] == jnp.arange(frames)[None, :]).astype(jnp.float32)
    pred_local = jnp.dot(site_energy, member, precision=hi) / FR
    grads = jnp.einsum("af,ai,aj->fij", member, desc, slope, precision=hi) / FR
    width = grads.shape[1] * grads.shape[2]
    grads = grads.reshape(frames, width)
    n_row = lax.axis_size("row")
    n_col = lax.axis_size("col")
    row_id = lax.axis_index("row")
    col_id = lax.axis_index("col")
    m_all = frames * n_row * n_col
    col_w = width // n_col
    blk = width // (n_row * n_col)
    col_part = shift_all_to_all(grads.reshape(frames, n_col, col_w), "col", n_col, col_id)
    grad_col = doubling_gather(col_part.reshape(n_col * frames, col_w), "row", n_row, row_id)
    nbits = n_col.bit_length() - 1
    letters = "abcdefgh"[:nbits]
    cov_blocks = cov.reshape((2,) * nbits + (cov.shape[0] // n_col, cov.shape[1]))
    partial_t = jnp.einsum(
        "mk," + letters + "ik->" + letters[::-1] + "mi", grad_col, cov_blocks, precision=mid
    )
    gain_own_t = halving_scatter(partial_t, "col", n_col, col_id)
    gain_rows_t = lax.all_gather(gain_own_t, "col", axis=1, tiled=True)
    factor = n_col // n_row
    half_t = lax.dynamic_slice_in_dim(gain_rows_t, col_id % factor * col_w, col_w, 1)
    mine = row_id == col_id // factor
    gram_part = jnp.einsum("mk,nk->mn", grad_col, half_t, precision=hi)
    gram_part = jnp.where(mine, gram_part, jnp.zeros_like(gram_part))
    device_id = row_id * n_col + col_id
    slots = lax.dynamic_update_slice_in_dim(
        jnp.zeros((8, m_all), jnp.float32),
        jnp.zeros((8, frames), jnp.float32).at[0].set(pred_local),
        device_id * frames,
        1,
    )
    small = jnp.concatenate([gram_part, slots], axis=0)
    small = butterfly_sum(butterfly_sum(small, "col", n_col), "row", n_row)
    masked = jnp.where(mine, half_t, jnp.zeros_like(half_t))
    small, masked = lax.optimization_barrier((small, masked))
    gram = small[:m_all] + jnp.diag(noise)
    pred_all = small[m_all]
    lower = jnp.linalg.cholesky(gram)
    gain_col_t = broadcast_rows(masked, n_row, n_col, factor)
    white_row = jax.scipy.linalg.solve_triangular(lower, gain_rows_t, lower=True)
    white_col = jax.scipy.linalg.solve_triangular(lower, gain_col_t, lower=True)
    new_cov = cov - jnp.einsum("mi,mj->ij", white_row, white_col, precision=mid)
    coef = jax.scipy.linalg.cho_solve((lower, True), targets - pred_all)
    own_weights = lax.dynamic_slice_in_dim(weights.reshape(-1), device_id * blk, blk, 0)
    new_weights = own_weights + jnp.dot(coef, gain_own_t, precision=hi)
    return (new_weights, new_cov)


def solution(mesh):
    return jax.shard_map(
        on_device,
        mesh=mesh,
        in_specs=(
            P(("row", "col"), None),
            P(("row", "col")),
            P(("row", "col"), None),
            P(("row", "col")),
            P(),
            P(),
            P(),
            P(),
            P(),
            P("row", "col"),
        ),
        out_specs=(P(("row", "col")), P("row", "col")),
        check_vma=False,
    )
```

```python
import jax
import jax.numpy as jnp
from jax import lax
from jax.sharding import PartitionSpec as P

FR = 64


def broadcast_rows(buf, n_row, n_col, factor):
    bits = []
    b = 1
    while b < n_row:
        bits.append(b)
        b *= 2
    bits = bits[1:][::-1] + bits[:1]
    held = [0]
    for bit in bits:
        perm = []
        for c in range(n_col):
            s = c // factor
            for rel in held:
                perm.append(((s ^ rel) * n_col + c, (s ^ rel ^ bit) * n_col + c))
        buf = buf + lax.ppermute(buf, ("row", "col"), perm)
        held = held + [rel ^ bit for rel in held]
    return buf


def butterfly_sum(buf, axis, size):
    bit = 1
    while bit < size:
        buf = buf + lax.ppermute(buf, axis, [(i, i ^ bit) for i in range(size)])
        bit *= 2
    return buf


def halving_scatter(x, axis, size, me):
    nbits = size.bit_length() - 1
    for step in range(nbits):
        bit = 1 << step
        mine = (me // bit) % 2
        keep = lax.dynamic_index_in_dim(x, mine, 0, keepdims=False)
        send = lax.dynamic_index_in_dim(x, 1 - mine, 0, keepdims=False)
        x = keep + lax.ppermute(send, axis, [(i, i ^ bit) for i in range(size)])
    return x


def shift_all_to_all(x, axis, size, me):
    got = [lax.dynamic_index_in_dim(x, me, 1, keepdims=False)]
    for k in range(1, size):
        piece = lax.dynamic_index_in_dim(x, (me + size - k) % size, 1, keepdims=False)
        got.append(lax.ppermute(piece, axis, [(i, (i - k) % size) for i in range(size)]))
    got = jnp.stack(got, axis=0)
    both = jnp.concatenate([got, got], axis=0)
    ordered = lax.dynamic_slice_in_dim(both, (size - me) % size, size, 0)
    return ordered.reshape((size * x.shape[0],) + x.shape[2:])


def doubling_gather(x, axis, size, me):
    bits = []
    bit = 1
    while bit < size:
        bits.append(bit)
        bit *= 2
    rows = x.shape[0]
    x = x[None]
    for bit in bits[::-1]:
        other = lax.ppermute(x, axis, [(i, i ^ bit) for i in range(size)])
        low = (me // bit) % 2 == 0
        x = jnp.where(low, jnp.stack([x, other], axis=1), jnp.stack([other, x], axis=1))
        x = x.reshape((x.shape[0] * 2,) + x.shape[2:])
    return x.reshape((size * rows,) + x.shape[2:])


def on_device(
    atom_feat, types, neighbors, frame_of_atom, weights, type_gain, out_vec, targets, noise, cov
):
    hi = lax.Precision.HIGHEST
    mid = lax.Precision.HIGH
    atoms = atom_feat.shape[0]
    ntypes = type_gain.shape[0]
    nbrs = neighbors.shape[1]
    frames = atoms // FR
    onehot_type = (types[:, None] == jnp.arange(ntypes)[None, :]).astype(jnp.float32)
    row_gain = jnp.dot(onehot_type, type_gain, precision=hi)
    row_out = jnp.dot(onehot_type, out_vec, precision=hi)
    scaled = atom_feat * row_gain
    counts = jnp.sum(
        (neighbors[:, :, None] == jnp.arange(atoms)[None, None, :]).astype(jnp.float32), axis=1
    )
    near_sum = jnp.dot(counts, scaled, precision=hi)
    desc = jnp.tanh(atom_feat + near_sum / nbrs)
    act = jnp.tanh(jnp.dot(desc, weights, precision=hi))
    site_energy = jnp.sum(act * row_out, axis=1)
    slope = (1.0 - act * act) * row_out
    member = (frame_of_atom[:, None] == jnp.arange(frames)[None, :]).astype(jnp.float32)
    pred_local = jnp.dot(site_energy, member, precision=hi) / FR
    grads = jnp.einsum("af,ai,aj->fij", member, desc, slope, precision=hi) / FR
    width = grads.shape[1] * grads.shape[2]
    grads = grads.reshape(frames, width)
    n_row = lax.axis_size("row")
    n_col = lax.axis_size("col")
    row_id = lax.axis_index("row")
    col_id = lax.axis_index("col")
    m_all = frames * n_row * n_col
    col_w = width // n_col
    blk = width // (n_row * n_col)
    col_part = shift_all_to_all(grads.reshape(frames, n_col, col_w), "col", n_col, col_id)
    grad_col = doubling_gather(col_part.reshape(n_col * frames, col_w), "row", n_row, row_id)
    nbits = n_col.bit_length() - 1
    letters = "abcdefgh"[:nbits]
    cov_blocks = cov.reshape((2,) * nbits + (cov.shape[0] // n_col, cov.shape[1]))
    partial_t = jnp.einsum(
        "mk," + letters + "ik->" + letters[::-1] + "mi", grad_col, cov_blocks, precision=mid
    )
    factor = n_col // n_row
    grad_own = None
    for t in range(n_row):
        perm = []
        for r in range(n_row):
            for q in range(factor):
                perm.append((r * n_col + r * factor + q, r * n_col + q * n_row + t))
        got = lax.ppermute(grad_col[:, t * blk : (t + 1) * blk], ("row", "col"), perm)
        grad_own = got if grad_own is None else grad_own + got
    grad_own, partial_t = lax.optimization_barrier((grad_own, partial_t))
    gain_own_t = halving_scatter(partial_t, "col", n_col, col_id)
    gram_own = jnp.einsum("mk,nk->mn", grad_own, gain_own_t, precision=hi)
    device_id = row_id * n_col + col_id
    slots = lax.dynamic_update_slice_in_dim(
        jnp.zeros((8, m_all), jnp.float32),
        jnp.zeros((8, frames), jnp.float32).at[0].set(pred_local),
        device_id * frames,
        1,
    )
    small = jnp.concatenate([gram_own, slots], axis=0)
    small = butterfly_sum(butterfly_sum(small, "col", n_col), "row", n_row)
    gain_rows_t = lax.all_gather(gain_own_t, "col", axis=1, tiled=True)
    half_t = lax.dynamic_slice_in_dim(gain_rows_t, col_id % factor * col_w, col_w, 1)
    mine = row_id == col_id // factor
    masked = jnp.where(mine, half_t, jnp.zeros_like(half_t))
    gram = small[:m_all] + jnp.diag(noise)
    pred_all = small[m_all]
    lower = jnp.linalg.cholesky(gram)
    gain_col_t = broadcast_rows(masked, n_row, n_col, factor)
    white_row = jax.scipy.linalg.solve_triangular(lower, gain_rows_t, lower=True)
    white_col = jax.scipy.linalg.solve_triangular(lower, gain_col_t, lower=True)
    new_cov = cov - jnp.einsum("mi,mj->ij", white_row, white_col, precision=mid)
    coef = jax.scipy.linalg.cho_solve((lower, True), targets - pred_all)
    own_weights = lax.dynamic_slice_in_dim(weights.reshape(-1), device_id * blk, blk, 0)
    new_weights = own_weights + jnp.dot(coef, gain_own_t, precision=hi)
    return (new_weights, new_cov)


def solution(mesh):
    return jax.shard_map(
        on_device,
        mesh=mesh,
        in_specs=(
            P(("row", "col"), None),
            P(("row", "col")),
            P(("row", "col"), None),
            P(("row", "col")),
            P(),
            P(),
            P(),
            P(),
            P(),
            P("row", "col"),
        ),
        out_specs=(P(("row", "col")), P("row", "col")),
        check_vma=False,
    )
```

```python
import jax
import jax.numpy as jnp
from jax import lax
from jax.sharding import PartitionSpec as P

FR = 64


def broadcast_rows(buf, n_row, n_col, factor):
    bits = []
    b = 1
    while b < n_row:
        bits.append(b)
        b *= 2
    bits = bits[1:][::-1] + bits[:1]
    held = [0]
    for bit in bits:
        perm = []
        for c in range(n_col):
            s = c // factor
            for rel in held:
                perm.append(((s ^ rel) * n_col + c, (s ^ rel ^ bit) * n_col + c))
        buf = buf + lax.ppermute(buf, ("row", "col"), perm)
        held = held + [rel ^ bit for rel in held]
    return buf


def butterfly_sum(buf, axis, size):
    bit = 1
    while bit < size:
        buf = buf + lax.ppermute(buf, axis, [(i, i ^ bit) for i in range(size)])
        bit *= 2
    return buf


def halving_scatter(x, axis, size, me):
    nbits = size.bit_length() - 1
    for step in range(nbits):
        bit = 1 << step
        mine = (me // bit) % 2
        keep = lax.dynamic_index_in_dim(x, mine, 0, keepdims=False)
        send = lax.dynamic_index_in_dim(x, 1 - mine, 0, keepdims=False)
        x = keep + lax.ppermute(send, axis, [(i, i ^ bit) for i in range(size)])
    return x


def shift_all_to_all(x, axis, size, me):
    got = [lax.dynamic_index_in_dim(x, me, 1, keepdims=False)]
    for k in range(1, size):
        piece = lax.dynamic_index_in_dim(x, (me + size - k) % size, 1, keepdims=False)
        got.append(lax.ppermute(piece, axis, [(i, (i - k) % size) for i in range(size)]))
    got = jnp.stack(got, axis=0)
    both = jnp.concatenate([got, got], axis=0)
    ordered = lax.dynamic_slice_in_dim(both, (size - me) % size, size, 0)
    return ordered.reshape((size * x.shape[0],) + x.shape[2:])


def doubling_gather(x, axis, size, me):
    bits = []
    bit = 1
    while bit < size:
        bits.append(bit)
        bit *= 2
    rows = x.shape[0]
    x = x[None]
    for bit in bits[::-1]:
        other = lax.ppermute(x, axis, [(i, i ^ bit) for i in range(size)])
        low = (me // bit) % 2 == 0
        x = jnp.where(low, jnp.stack([x, other], axis=1), jnp.stack([other, x], axis=1))
        x = x.reshape((x.shape[0] * 2,) + x.shape[2:])
    return x.reshape((size * rows,) + x.shape[2:])


def on_device(
    atom_feat, types, neighbors, frame_of_atom, weights, type_gain, out_vec, targets, noise, cov
):
    hi = lax.Precision.HIGHEST
    mid = lax.Precision.HIGH
    atoms = atom_feat.shape[0]
    ntypes = type_gain.shape[0]
    nbrs = neighbors.shape[1]
    frames = atoms // FR
    onehot_type = (types[:, None] == jnp.arange(ntypes)[None, :]).astype(jnp.float32)
    row_gain = jnp.dot(onehot_type, type_gain, precision=hi)
    row_out = jnp.dot(onehot_type, out_vec, precision=hi)
    scaled = atom_feat * row_gain
    counts = jnp.sum(
        (neighbors[:, :, None] == jnp.arange(atoms)[None, None, :]).astype(jnp.float32), axis=1
    )
    near_sum = jnp.dot(counts, scaled, precision=hi)
    desc = jnp.tanh(atom_feat + near_sum / nbrs)
    act = jnp.tanh(jnp.dot(desc, weights, precision=hi))
    site_energy = jnp.sum(act * row_out, axis=1)
    slope = (1.0 - act * act) * row_out
    member = (frame_of_atom[:, None] == jnp.arange(frames)[None, :]).astype(jnp.float32)
    pred_local = jnp.dot(site_energy, member, precision=hi) / FR
    grads = jnp.einsum("af,ai,aj->fij", member, desc, slope, precision=hi) / FR
    width = grads.shape[1] * grads.shape[2]
    grads = grads.reshape(frames, width)
    n_row = lax.axis_size("row")
    n_col = lax.axis_size("col")
    row_id = lax.axis_index("row")
    col_id = lax.axis_index("col")
    m_all = frames * n_row * n_col
    col_w = width // n_col
    blk = width // (n_row * n_col)
    col_part = shift_all_to_all(grads.reshape(frames, n_col, col_w), "col", n_col, col_id)
    grad_col = doubling_gather(col_part.reshape(n_col * frames, col_w), "row", n_row, row_id)
    nbits = n_col.bit_length() - 1
    letters = "abcdefgh"[:nbits]
    cov_blocks = cov.reshape((2,) * nbits + (cov.shape[0] // n_col, cov.shape[1]))
    partial_t = jnp.einsum(
        "mk," + letters + "ik->" + letters[::-1] + "mi", grad_col, cov_blocks, precision=mid
    )
    factor = n_col // n_row
    grad_own = None
    for t in range(n_row):
        perm = []
        for r in range(n_row):
            for q in range(factor):
                perm.append((r * n_col + r * factor + q, r * n_col + q * n_row + t))
        got = lax.ppermute(grad_col[:, t * blk : (t + 1) * blk], ("row", "col"), perm)
        grad_own = got if grad_own is None else grad_own + got
    grad_own, partial_t = lax.optimization_barrier((grad_own, partial_t))
    gain_own_t = halving_scatter(partial_t, "col", n_col, col_id)
    gram_own = jnp.einsum("mk,nk->mn", grad_own, gain_own_t, precision=hi)
    device_id = row_id * n_col + col_id
    slots = lax.dynamic_update_slice_in_dim(
        jnp.zeros((8, m_all), jnp.float32),
        jnp.zeros((8, frames), jnp.float32).at[0].set(pred_local),
        device_id * frames,
        1,
    )
    small = jnp.concatenate([gram_own, slots], axis=0)
    small = butterfly_sum(butterfly_sum(small, "col", n_col), "row", n_row)
    gain_rows_t = lax.all_gather(gain_own_t, "col", axis=1, tiled=True)
    half_t = lax.dynamic_slice_in_dim(gain_rows_t, col_id % factor * col_w, col_w, 1)
    mine = row_id == col_id // factor
    masked = jnp.where(mine, half_t, jnp.zeros_like(half_t))
    small, masked = lax.optimization_barrier((small, masked))
    gram = small[:m_all] + jnp.diag(noise)
    pred_all = small[m_all]
    lower = jnp.linalg.cholesky(gram)
    gain_col_t = broadcast_rows(masked, n_row, n_col, factor)
    white_row = jax.scipy.linalg.solve_triangular(lower, gain_rows_t, lower=True)
    white_col = jax.scipy.linalg.solve_triangular(lower, gain_col_t, lower=True)
    new_cov = cov - jnp.einsum("mi,mj->ij", white_row, white_col, precision=mid)
    coef = jax.scipy.linalg.cho_solve((lower, True), targets - pred_all)
    own_weights = lax.dynamic_slice_in_dim(weights.reshape(-1), device_id * blk, blk, 0)
    new_weights = own_weights + jnp.dot(coef, gain_own_t, precision=hi)
    return (new_weights, new_cov)


def solution(mesh):
    return jax.shard_map(
        on_device,
        mesh=mesh,
        in_specs=(
            P(("row", "col"), None),
            P(("row", "col")),
            P(("row", "col"), None),
            P(("row", "col")),
            P(),
            P(),
            P(),
            P(),
            P(),
            P("row", "col"),
        ),
        out_specs=(P(("row", "col")), P("row", "col")),
        check_vma=False,
    )
```

```python
import jax
import jax.numpy as jnp
from jax import lax
from jax.sharding import PartitionSpec as P

FR = 64


def broadcast_rows(buf, n_row, n_col, factor):
    bits = []
    b = 1
    while b < n_row:
        bits.append(b)
        b *= 2
    bits = bits[1:][::-1] + bits[:1]
    held = [0]
    for bit in bits:
        perm = []
        for c in range(n_col):
            s = c // factor
            for rel in held:
                perm.append(((s ^ rel) * n_col + c, (s ^ rel ^ bit) * n_col + c))
        buf = buf + lax.ppermute(buf, ("row", "col"), perm)
        held = held + [rel ^ bit for rel in held]
    return buf


def butterfly_sum(buf, axis, size):
    bit = 1
    while bit < size:
        buf = buf + lax.ppermute(buf, axis, [(i, i ^ bit) for i in range(size)])
        bit *= 2
    return buf


def halving_scatter(x, axis, size, me):
    nbits = size.bit_length() - 1
    for step in range(nbits):
        bit = 1 << step
        mine = (me // bit) % 2
        keep = lax.dynamic_index_in_dim(x, mine, 0, keepdims=False)
        send = lax.dynamic_index_in_dim(x, 1 - mine, 0, keepdims=False)
        x = keep + lax.ppermute(send, axis, [(i, i ^ bit) for i in range(size)])
    return x


def shift_all_to_all(x, axis, size, me):
    got = [lax.dynamic_index_in_dim(x, me, 1, keepdims=False)]
    for k in range(1, size):
        piece = lax.dynamic_index_in_dim(x, (me + size - k) % size, 1, keepdims=False)
        got.append(lax.ppermute(piece, axis, [(i, (i - k) % size) for i in range(size)]))
    got = jnp.stack(got, axis=0)
    both = jnp.concatenate([got, got], axis=0)
    ordered = lax.dynamic_slice_in_dim(both, (size - me) % size, size, 0)
    return ordered.reshape((size * x.shape[0],) + x.shape[2:])


def doubling_gather(x, axis, size, me):
    bits = []
    bit = 1
    while bit < size:
        bits.append(bit)
        bit *= 2
    rows = x.shape[0]
    x = x[None]
    for bit in bits[::-1]:
        other = lax.ppermute(x, axis, [(i, i ^ bit) for i in range(size)])
        low = (me // bit) % 2 == 0
        x = jnp.where(low, jnp.stack([x, other], axis=1), jnp.stack([other, x], axis=1))
        x = x.reshape((x.shape[0] * 2,) + x.shape[2:])
    return x.reshape((size * rows,) + x.shape[2:])


def on_device(
    atom_feat, types, neighbors, frame_of_atom, weights, type_gain, out_vec, targets, noise, cov
):
    hi = lax.Precision.HIGHEST
    mid = lax.Precision.HIGH
    atoms = atom_feat.shape[0]
    ntypes = type_gain.shape[0]
    nbrs = neighbors.shape[1]
    frames = atoms // FR
    onehot_type = (types[:, None] == jnp.arange(ntypes)[None, :]).astype(jnp.float32)
    row_gain = jnp.dot(onehot_type, type_gain, precision=hi)
    row_out = jnp.dot(onehot_type, out_vec, precision=hi)
    scaled = atom_feat * row_gain
    counts = jnp.sum(
        (neighbors[:, :, None] == jnp.arange(atoms)[None, None, :]).astype(jnp.float32), axis=1
    )
    near_sum = jnp.dot(counts, scaled, precision=hi)
    desc = jnp.tanh(atom_feat + near_sum / nbrs)
    act = jnp.tanh(jnp.dot(desc, weights, precision=hi))
    site_energy = jnp.sum(act * row_out, axis=1)
    slope = (1.0 - act * act) * row_out
    member = (frame_of_atom[:, None] == jnp.arange(frames)[None, :]).astype(jnp.float32)
    pred_local = jnp.dot(site_energy, member, precision=hi) / FR
    grads = jnp.einsum("af,ai,aj->fij", member, desc, slope, precision=hi) / FR
    width = grads.shape[1] * grads.shape[2]
    grads = grads.reshape(frames, width)
    n_row = lax.axis_size("row")
    n_col = lax.axis_size("col")
    row_id = lax.axis_index("row")
    col_id = lax.axis_index("col")
    m_all = frames * n_row * n_col
    col_w = width // n_col
    blk = width // (n_row * n_col)
    col_part = shift_all_to_all(grads.reshape(frames, n_col, col_w), "col", n_col, col_id)
    grad_col = doubling_gather(col_part.reshape(n_col * frames, col_w), "row", n_row, row_id)
    nbits = n_col.bit_length() - 1
    letters = "abcdefgh"[:nbits]
    cov_blocks = cov.reshape((2,) * nbits + (cov.shape[0] // n_col, cov.shape[1]))
    partial_t = jnp.einsum(
        "mk," + letters + "ik->" + letters[::-1] + "mi", grad_col, cov_blocks, precision=mid
    )
    factor = n_col // n_row
    grad_own = None
    for t in range(n_row):
        perm = []
        for r in range(n_row):
            for q in range(factor):
                perm.append((r * n_col + r * factor + q, r * n_col + q * n_row + t))
        got = lax.ppermute(grad_col[:, t * blk : (t + 1) * blk], ("row", "col"), perm)
        grad_own = got if grad_own is None else grad_own + got
    grad_own, partial_t = lax.optimization_barrier((grad_own, partial_t))
    gain_own_t = halving_scatter(partial_t, "col", n_col, col_id)
    gram_own = jnp.einsum("mk,nk->mn", grad_own, gain_own_t, precision=hi)
    device_id = row_id * n_col + col_id
    slots = lax.dynamic_update_slice_in_dim(
        jnp.zeros((8, m_all), jnp.float32),
        jnp.zeros((8, frames), jnp.float32).at[0].set(pred_local),
        device_id * frames,
        1,
    )
    small = jnp.concatenate([gram_own, slots], axis=0)
    small = butterfly_sum(butterfly_sum(small, "col", n_col), "row", n_row)
    gain_rows_t = lax.all_gather(gain_own_t, "col", axis=1, tiled=True)
    gram = small[:m_all] + jnp.diag(noise)
    pred_all = small[m_all]
    lower = jnp.linalg.cholesky(gram)
    lower, gain_rows_t = lax.optimization_barrier((lower, gain_rows_t))
    half_t = lax.dynamic_slice_in_dim(gain_rows_t, col_id % factor * col_w, col_w, 1)
    mine = row_id == col_id // factor
    masked = jnp.where(mine, half_t, jnp.zeros_like(half_t))
    gain_col_t = broadcast_rows(masked, n_row, n_col, factor)
    white_row = jax.scipy.linalg.solve_triangular(lower, gain_rows_t, lower=True)
    white_col = jax.scipy.linalg.solve_triangular(lower, gain_col_t, lower=True)
    new_cov = cov - jnp.einsum("mi,mj->ij", white_row, white_col, precision=mid)
    coef = jax.scipy.linalg.cho_solve((lower, True), targets - pred_all)
    own_weights = lax.dynamic_slice_in_dim(weights.reshape(-1), device_id * blk, blk, 0)
    new_weights = own_weights + jnp.dot(coef, gain_own_t, precision=hi)
    return (new_weights, new_cov)


def solution(mesh):
    return jax.shard_map(
        on_device,
        mesh=mesh,
        in_specs=(
            P(("row", "col"), None),
            P(("row", "col")),
            P(("row", "col"), None),
            P(("row", "col")),
            P(),
            P(),
            P(),
            P(),
            P(),
            P("row", "col"),
        ),
        out_specs=(P(("row", "col")), P("row", "col")),
        check_vma=False,
    )
```

```python
import jax
import jax.numpy as jnp
from jax import lax
from jax.sharding import PartitionSpec as P

FR = 64


def broadcast_rows(buf, n_row, n_col, factor):
    bits = []
    b = 1
    while b < n_row:
        bits.append(b)
        b *= 2
    bits = bits[1:][::-1] + bits[:1]
    held = [0]
    for bit in bits:
        perm = []
        for c in range(n_col):
            s = c // factor
            for rel in held:
                perm.append(((s ^ rel) * n_col + c, (s ^ rel ^ bit) * n_col + c))
        buf = buf + lax.ppermute(buf, ("row", "col"), perm)
        held = held + [rel ^ bit for rel in held]
    return buf


def butterfly_sum(buf, axis, size):
    bit = 1
    while bit < size:
        buf = buf + lax.ppermute(buf, axis, [(i, i ^ bit) for i in range(size)])
        bit *= 2
    return buf


def halving_scatter(x, axis, size, me, done=0):
    nbits = size.bit_length() - 1
    for step in range(done, nbits):
        bit = 1 << step
        mine = (me // bit) % 2
        keep = lax.dynamic_index_in_dim(x, mine, 0, keepdims=False)
        send = lax.dynamic_index_in_dim(x, 1 - mine, 0, keepdims=False)
        x = keep + lax.ppermute(send, axis, [(i, i ^ bit) for i in range(size)])
    return x


def shift_all_to_all(x, axis, size, me):
    got = [lax.dynamic_index_in_dim(x, me, 1, keepdims=False)]
    for k in range(1, size):
        piece = lax.dynamic_index_in_dim(x, (me + size - k) % size, 1, keepdims=False)
        got.append(lax.ppermute(piece, axis, [(i, (i - k) % size) for i in range(size)]))
    got = jnp.stack(got, axis=0)
    both = jnp.concatenate([got, got], axis=0)
    ordered = lax.dynamic_slice_in_dim(both, (size - me) % size, size, 0)
    return ordered.reshape((size * x.shape[0],) + x.shape[2:])


def doubling_gather(x, axis, size, me):
    bits = []
    bit = 1
    while bit < size:
        bits.append(bit)
        bit *= 2
    rows = x.shape[0]
    x = x[None]
    for bit in bits[::-1]:
        other = lax.ppermute(x, axis, [(i, i ^ bit) for i in range(size)])
        low = (me // bit) % 2 == 0
        x = jnp.where(low, jnp.stack([x, other], axis=1), jnp.stack([other, x], axis=1))
        x = x.reshape((x.shape[0] * 2,) + x.shape[2:])
    return x.reshape((size * rows,) + x.shape[2:])


def on_device(
    atom_feat, types, neighbors, frame_of_atom, weights, type_gain, out_vec, targets, noise, cov
):
    hi = lax.Precision.HIGHEST
    mid = lax.Precision.HIGH
    atoms = atom_feat.shape[0]
    ntypes = type_gain.shape[0]
    nbrs = neighbors.shape[1]
    frames = atoms // FR
    onehot_type = (types[:, None] == jnp.arange(ntypes)[None, :]).astype(jnp.float32)
    row_gain = jnp.dot(onehot_type, type_gain, precision=hi)
    row_out = jnp.dot(onehot_type, out_vec, precision=hi)
    scaled = atom_feat * row_gain
    counts = jnp.sum(
        (neighbors[:, :, None] == jnp.arange(atoms)[None, None, :]).astype(jnp.float32), axis=1
    )
    near_sum = jnp.dot(counts, scaled, precision=hi)
    desc = jnp.tanh(atom_feat + near_sum / nbrs)
    act = jnp.tanh(jnp.dot(desc, weights, precision=hi))
    site_energy = jnp.sum(act * row_out, axis=1)
    slope = (1.0 - act * act) * row_out
    member = (frame_of_atom[:, None] == jnp.arange(frames)[None, :]).astype(jnp.float32)
    pred_local = jnp.dot(site_energy, member, precision=hi) / FR
    grads = jnp.einsum("af,ai,aj->fij", member, desc, slope, precision=hi) / FR
    width = grads.shape[1] * grads.shape[2]
    grads = grads.reshape(frames, width)
    n_row = lax.axis_size("row")
    n_col = lax.axis_size("col")
    row_id = lax.axis_index("row")
    col_id = lax.axis_index("col")
    m_all = frames * n_row * n_col
    col_w = width // n_col
    blk = width // (n_row * n_col)
    col_part = shift_all_to_all(grads.reshape(frames, n_col, col_w), "col", n_col, col_id)
    grad_col = doubling_gather(col_part.reshape(n_col * frames, col_w), "row", n_row, row_id)
    nbits = n_col.bit_length() - 1
    letters = "abcdefgh"[:nbits]
    cov_blocks = cov.reshape((2,) * nbits + (cov.shape[0] // n_col, cov.shape[1]))
    first = col_id % 2
    spec = "mk," + letters[:-1] + "ik->" + letters[:-1][::-1] + "mi"
    send_rows = lax.dynamic_index_in_dim(cov_blocks, 1 - first, nbits - 1, keepdims=False)
    send_part = jnp.einsum(spec, grad_col, send_rows, precision=mid)
    got_part = lax.ppermute(send_part, "col", [(i, i ^ 1) for i in range(n_col)])
    keep_rows = lax.dynamic_index_in_dim(cov_blocks, first, nbits - 1, keepdims=False)
    keep_part = jnp.einsum(spec, grad_col, keep_rows, precision=mid)
    partial_t = keep_part + got_part
    factor = n_col // n_row
    grad_own = None
    for t in range(n_row):
        perm = []
        for r in range(n_row):
            for q in range(factor):
                perm.append((r * n_col + r * factor + q, r * n_col + q * n_row + t))
        got = lax.ppermute(grad_col[:, t * blk : (t + 1) * blk], ("row", "col"), perm)
        grad_own = got if grad_own is None else grad_own + got
    grad_own, partial_t = lax.optimization_barrier((grad_own, partial_t))
    gain_own_t = halving_scatter(partial_t, "col", n_col, col_id, 1)
    gram_own = jnp.einsum("mk,nk->mn", grad_own, gain_own_t, precision=hi)
    device_id = row_id * n_col + col_id
    slots = lax.dynamic_update_slice_in_dim(
        jnp.zeros((8, m_all), jnp.float32),
        jnp.zeros((8, frames), jnp.float32).at[0].set(pred_local),
        device_id * frames,
        1,
    )
    small = jnp.concatenate([gram_own, slots], axis=0)
    small = butterfly_sum(butterfly_sum(small, "col", n_col), "row", n_row)
    gain_rows_t = lax.all_gather(gain_own_t, "col", axis=1, tiled=True)
    gram = small[:m_all] + jnp.diag(noise)
    pred_all = small[m_all]
    lower = jnp.linalg.cholesky(gram)
    lower, gain_rows_t = lax.optimization_barrier((lower, gain_rows_t))
    half_t = lax.dynamic_slice_in_dim(gain_rows_t, col_id % factor * col_w, col_w, 1)
    mine = row_id == col_id // factor
    masked = jnp.where(mine, half_t, jnp.zeros_like(half_t))
    gain_col_t = broadcast_rows(masked, n_row, n_col, factor)
    white_row = jax.scipy.linalg.solve_triangular(lower, gain_rows_t, lower=True)
    white_col = jax.scipy.linalg.solve_triangular(lower, gain_col_t, lower=True)
    new_cov = cov - jnp.einsum("mi,mj->ij", white_row, white_col, precision=mid)
    coef = jax.scipy.linalg.cho_solve((lower, True), targets - pred_all)
    own_weights = lax.dynamic_slice_in_dim(weights.reshape(-1), device_id * blk, blk, 0)
    new_weights = own_weights + jnp.dot(coef, gain_own_t, precision=hi)
    return (new_weights, new_cov)


def solution(mesh):
    return jax.shard_map(
        on_device,
        mesh=mesh,
        in_specs=(
            P(("row", "col"), None),
            P(("row", "col")),
            P(("row", "col"), None),
            P(("row", "col")),
            P(),
            P(),
            P(),
            P(),
            P(),
            P("row", "col"),
        ),
        out_specs=(P(("row", "col")), P("row", "col")),
        check_vma=False,
    )
```

```python
import jax
import jax.numpy as jnp
from jax import lax
from jax.sharding import PartitionSpec as P

FR = 64


def broadcast_rows(buf, n_row, n_col, factor):
    bits = []
    b = 1
    while b < n_row:
        bits.append(b)
        b *= 2
    bits = bits[1:][::-1] + bits[:1]
    held = [0]
    for bit in bits:
        perm = []
        for c in range(n_col):
            s = c // factor
            for rel in held:
                perm.append(((s ^ rel) * n_col + c, (s ^ rel ^ bit) * n_col + c))
        buf = buf + lax.ppermute(buf, ("row", "col"), perm)
        held = held + [rel ^ bit for rel in held]
    return buf


def butterfly_sum(buf, axis, size):
    bit = 1
    while bit < size:
        buf = buf + lax.ppermute(buf, axis, [(i, i ^ bit) for i in range(size)])
        bit *= 2
    return buf


def halving_scatter(x, axis, size, me, done=0):
    nbits = size.bit_length() - 1
    for step in range(done, nbits):
        bit = 1 << step
        mine = (me // bit) % 2
        keep = lax.dynamic_index_in_dim(x, mine, 0, keepdims=False)
        send = lax.dynamic_index_in_dim(x, 1 - mine, 0, keepdims=False)
        x = keep + lax.ppermute(send, axis, [(i, i ^ bit) for i in range(size)])
    return x


def shift_all_to_all(x, axis, size, me):
    got = [lax.dynamic_index_in_dim(x, me, 1, keepdims=False)]
    for k in range(1, size):
        piece = lax.dynamic_index_in_dim(x, (me + size - k) % size, 1, keepdims=False)
        got.append(lax.ppermute(piece, axis, [(i, (i - k) % size) for i in range(size)]))
    got = jnp.stack(got, axis=0)
    both = jnp.concatenate([got, got], axis=0)
    ordered = lax.dynamic_slice_in_dim(both, (size - me) % size, size, 0)
    return ordered.reshape((size * x.shape[0],) + x.shape[2:])


def doubling_gather(x, axis, size, me):
    bits = []
    bit = 1
    while bit < size:
        bits.append(bit)
        bit *= 2
    rows = x.shape[0]
    x = x[None]
    for bit in bits[::-1]:
        other = lax.ppermute(x, axis, [(i, i ^ bit) for i in range(size)])
        low = (me // bit) % 2 == 0
        x = jnp.where(low, jnp.stack([x, other], axis=1), jnp.stack([other, x], axis=1))
        x = x.reshape((x.shape[0] * 2,) + x.shape[2:])
    return x.reshape((size * rows,) + x.shape[2:])


def on_device(
    atom_feat, types, neighbors, frame_of_atom, weights, type_gain, out_vec, targets, noise, cov
):
    hi = lax.Precision.HIGHEST
    mid = lax.Precision.HIGH
    atoms = atom_feat.shape[0]
    ntypes = type_gain.shape[0]
    nbrs = neighbors.shape[1]
    frames = atoms // FR
    onehot_type = (types[:, None] == jnp.arange(ntypes)[None, :]).astype(jnp.float32)
    row_gain = jnp.dot(onehot_type, type_gain, precision=hi)
    row_out = jnp.dot(onehot_type, out_vec, precision=hi)
    scaled = atom_feat * row_gain
    counts = jnp.sum(
        (neighbors[:, :, None] == jnp.arange(atoms)[None, None, :]).astype(jnp.float32), axis=1
    )
    near_sum = jnp.dot(counts, scaled, precision=hi)
    desc = jnp.tanh(atom_feat + near_sum / nbrs)
    act = jnp.tanh(jnp.dot(desc, weights, precision=hi))
    site_energy = jnp.sum(act * row_out, axis=1)
    slope = (1.0 - act * act) * row_out
    member = (frame_of_atom[:, None] == jnp.arange(frames)[None, :]).astype(jnp.float32)
    pred_local = jnp.dot(site_energy, member, precision=hi) / FR
    grads = jnp.einsum("af,ai,aj->fij", member, desc, slope, precision=hi) / FR
    width = grads.shape[1] * grads.shape[2]
    grads = grads.reshape(frames, width)
    n_row = lax.axis_size("row")
    n_col = lax.axis_size("col")
    row_id = lax.axis_index("row")
    col_id = lax.axis_index("col")
    m_all = frames * n_row * n_col
    col_w = width // n_col
    blk = width // (n_row * n_col)
    col_part = shift_all_to_all(grads.reshape(frames, n_col, col_w), "col", n_col, col_id)
    grad_col = doubling_gather(col_part.reshape(n_col * frames, col_w), "row", n_row, row_id)
    nbits = n_col.bit_length() - 1
    letters = "abcdefgh"[:nbits]
    cov_blocks = cov.reshape((2,) * nbits + (cov.shape[0] // n_col, cov.shape[1]))
    first = col_id % 2
    spec = "mk," + letters[:-1] + "ik->" + letters[:-1][::-1] + "mi"
    send_rows = lax.dynamic_index_in_dim(cov_blocks, 1 - first, nbits - 1, keepdims=False)
    send_part = jnp.einsum(spec, grad_col, send_rows, precision=mid)
    got_part = lax.ppermute(send_part, "col", [(i, i ^ 1) for i in range(n_col)])
    keep_rows = lax.dynamic_index_in_dim(cov_blocks, first, nbits - 1, keepdims=False)
    keep_part = jnp.einsum(spec, grad_col, keep_rows, precision=mid)
    partial_t = (keep_part, got_part)
    factor = n_col // n_row
    grad_own = None
    for t in range(n_row):
        perm = []
        for r in range(n_row):
            for q in range(factor):
                perm.append((r * n_col + r * factor + q, r * n_col + q * n_row + t))
        got = lax.ppermute(grad_col[:, t * blk : (t + 1) * blk], ("row", "col"), perm)
        grad_own = got if grad_own is None else grad_own + got
    grad_own, keep_part = lax.optimization_barrier((grad_own, partial_t[0]))
    partial_t = keep_part + partial_t[1]
    gain_own_t = halving_scatter(partial_t, "col", n_col, col_id, 1)
    gram_own = jnp.einsum("mk,nk->mn", grad_own, gain_own_t, precision=hi)
    device_id = row_id * n_col + col_id
    slots = lax.dynamic_update_slice_in_dim(
        jnp.zeros((8, m_all), jnp.float32),
        jnp.zeros((8, frames), jnp.float32).at[0].set(pred_local),
        device_id * frames,
        1,
    )
    small = jnp.concatenate([gram_own, slots], axis=0)
    small = butterfly_sum(butterfly_sum(small, "col", n_col), "row", n_row)
    gain_rows_t = lax.all_gather(gain_own_t, "col", axis=1, tiled=True)
    gram = small[:m_all] + jnp.diag(noise)
    pred_all = small[m_all]
    lower = jnp.linalg.cholesky(gram)
    lower, gain_rows_t = lax.optimization_barrier((lower, gain_rows_t))
    half_t = lax.dynamic_slice_in_dim(gain_rows_t, col_id % factor * col_w, col_w, 1)
    mine = row_id == col_id // factor
    masked = jnp.where(mine, half_t, jnp.zeros_like(half_t))
    gain_col_t = broadcast_rows(masked, n_row, n_col, factor)
    white_row = jax.scipy.linalg.solve_triangular(lower, gain_rows_t, lower=True)
    white_col = jax.scipy.linalg.solve_triangular(lower, gain_col_t, lower=True)
    new_cov = cov - jnp.einsum("mi,mj->ij", white_row, white_col, precision=mid)
    coef = jax.scipy.linalg.cho_solve((lower, True), targets - pred_all)
    own_weights = lax.dynamic_slice_in_dim(weights.reshape(-1), device_id * blk, blk, 0)
    new_weights = own_weights + jnp.dot(coef, gain_own_t, precision=hi)
    return (new_weights, new_cov)


def solution(mesh):
    return jax.shard_map(
        on_device,
        mesh=mesh,
        in_specs=(
            P(("row", "col"), None),
            P(("row", "col")),
            P(("row", "col"), None),
            P(("row", "col")),
            P(),
            P(),
            P(),
            P(),
            P(),
            P("row", "col"),
        ),
        out_specs=(P(("row", "col")), P("row", "col")),
        check_vma=False,
    )
```

```python
import jax
import jax.numpy as jnp
from jax import lax
from jax.sharding import PartitionSpec as P

FR = 64


def broadcast_rows(buf, n_row, n_col, factor):
    bits = []
    b = 1
    while b < n_row:
        bits.append(b)
        b *= 2
    bits = bits[1:][::-1] + bits[:1]
    held = [0]
    for bit in bits:
        perm = []
        for c in range(n_col):
            s = c // factor
            for rel in held:
                perm.append(((s ^ rel) * n_col + c, (s ^ rel ^ bit) * n_col + c))
        buf = buf + lax.ppermute(buf, ("row", "col"), perm)
        held = held + [rel ^ bit for rel in held]
    return buf


def butterfly_sum(buf, axis, size):
    bit = 1
    while bit < size:
        buf = buf + lax.ppermute(buf, axis, [(i, i ^ bit) for i in range(size)])
        bit *= 2
    return buf


def halving_scatter(x, axis, size, me, done=0):
    nbits = size.bit_length() - 1
    for step in range(done, nbits):
        bit = 1 << step
        mine = (me // bit) % 2
        keep = lax.dynamic_index_in_dim(x, mine, 0, keepdims=False)
        send = lax.dynamic_index_in_dim(x, 1 - mine, 0, keepdims=False)
        x = keep + lax.ppermute(send, axis, [(i, i ^ bit) for i in range(size)])
    return x


def shift_all_to_all(x, axis, size, me):
    got = [lax.dynamic_index_in_dim(x, me, 1, keepdims=False)]
    for k in range(1, size):
        piece = lax.dynamic_index_in_dim(x, (me + size - k) % size, 1, keepdims=False)
        got.append(lax.ppermute(piece, axis, [(i, (i - k) % size) for i in range(size)]))
    got = jnp.stack(got, axis=0)
    both = jnp.concatenate([got, got], axis=0)
    ordered = lax.dynamic_slice_in_dim(both, (size - me) % size, size, 0)
    return ordered.reshape((size * x.shape[0],) + x.shape[2:])


def doubling_gather(x, axis, size, me):
    bits = []
    bit = 1
    while bit < size:
        bits.append(bit)
        bit *= 2
    rows = x.shape[0]
    x = x[None]
    for bit in bits[::-1]:
        other = lax.ppermute(x, axis, [(i, i ^ bit) for i in range(size)])
        low = (me // bit) % 2 == 0
        x = jnp.where(low, jnp.stack([x, other], axis=1), jnp.stack([other, x], axis=1))
        x = x.reshape((x.shape[0] * 2,) + x.shape[2:])
    return x.reshape((size * rows,) + x.shape[2:])


def on_device(
    atom_feat, types, neighbors, frame_of_atom, weights, type_gain, out_vec, targets, noise, cov
):
    hi = lax.Precision.HIGHEST
    mid = lax.Precision.HIGH
    atoms = atom_feat.shape[0]
    ntypes = type_gain.shape[0]
    nbrs = neighbors.shape[1]
    frames = atoms // FR
    onehot_type = (types[:, None] == jnp.arange(ntypes)[None, :]).astype(jnp.float32)
    row_gain = jnp.dot(onehot_type, type_gain, precision=hi)
    row_out = jnp.dot(onehot_type, out_vec, precision=hi)
    scaled = atom_feat * row_gain
    counts = jnp.sum(
        (neighbors[:, :, None] == jnp.arange(atoms)[None, None, :]).astype(jnp.float32), axis=1
    )
    near_sum = jnp.dot(counts, scaled, precision=hi)
    desc = jnp.tanh(atom_feat + near_sum / nbrs)
    act = jnp.tanh(jnp.dot(desc, weights, precision=hi))
    site_energy = jnp.sum(act * row_out, axis=1)
    slope = (1.0 - act * act) * row_out
    member = (frame_of_atom[:, None] == jnp.arange(frames)[None, :]).astype(jnp.float32)
    pred_local = jnp.dot(site_energy, member, precision=hi) / FR
    grads = jnp.einsum("af,ai,aj->fij", member, desc, slope, precision=hi) / FR
    width = grads.shape[1] * grads.shape[2]
    grads = grads.reshape(frames, width)
    n_row = lax.axis_size("row")
    n_col = lax.axis_size("col")
    row_id = lax.axis_index("row")
    col_id = lax.axis_index("col")
    m_all = frames * n_row * n_col
    col_w = width // n_col
    blk = width // (n_row * n_col)
    col_part = shift_all_to_all(grads.reshape(frames, n_col, col_w), "col", n_col, col_id)
    grad_col = doubling_gather(col_part.reshape(n_col * frames, col_w), "row", n_row, row_id)
    nbits = n_col.bit_length() - 1
    letters = "abcdefgh"[:nbits]
    cov_blocks = cov.reshape((2,) * nbits + (cov.shape[0] // n_col, cov.shape[1]))
    first = col_id % 2
    spec = "mk," + letters[:-1] + "ik->" + letters[:-1][::-1] + "mi"
    send_rows = lax.dynamic_index_in_dim(cov_blocks, 1 - first, nbits - 1, keepdims=False)
    send_part = jnp.einsum(spec, grad_col, send_rows, precision=mid)
    got_part = lax.ppermute(send_part, "col", [(i, i ^ 1) for i in range(n_col)])
    keep_rows = lax.dynamic_index_in_dim(cov_blocks, first, nbits - 1, keepdims=False)
    keep_part = jnp.einsum(spec, grad_col, keep_rows, precision=mid)
    partial_t = (keep_part, got_part)
    factor = n_col // n_row
    grad_own = None
    for t in range(n_row):
        perm = []
        for r in range(n_row):
            for q in range(factor):
                perm.append((r * n_col + r * factor + q, r * n_col + q * n_row + t))
        got = lax.ppermute(grad_col[:, t * blk : (t + 1) * blk], ("row", "col"), perm)
        grad_own = got if grad_own is None else grad_own + got
    grad_own, keep_part = lax.optimization_barrier((grad_own, partial_t[0]))
    partial_t = keep_part + partial_t[1]
    gain_own_t = halving_scatter(partial_t, "col", n_col, col_id, 1)
    gram_own = jnp.einsum("mk,nk->mn", grad_own, gain_own_t, precision=hi)
    device_id = row_id * n_col + col_id
    slots = lax.dynamic_update_slice_in_dim(
        jnp.zeros((8, m_all), jnp.float32),
        jnp.zeros((8, frames), jnp.float32).at[0].set(pred_local),
        device_id * frames,
        1,
    )
    small = jnp.concatenate([gram_own, slots], axis=0)
    small = butterfly_sum(butterfly_sum(small, "col", n_col), "row", n_row)
    gain_rows_t = lax.all_gather(gain_own_t, "col", axis=1, tiled=True)
    gram = small[:m_all] + jnp.diag(noise)
    pred_all = small[m_all]
    lower = jnp.linalg.cholesky(gram)
    lower_inv = jax.scipy.linalg.solve_triangular(lower, jnp.eye(m_all, dtype=jnp.float32), lower=True)
    lower, lower_inv, gain_rows_t = lax.optimization_barrier((lower, lower_inv, gain_rows_t))
    half_t = lax.dynamic_slice_in_dim(gain_rows_t, col_id % factor * col_w, col_w, 1)
    mine = row_id == col_id // factor
    masked = jnp.where(mine, half_t, jnp.zeros_like(half_t))
    gain_col_t = broadcast_rows(masked, n_row, n_col, factor)
    white_row = jnp.dot(lower_inv, gain_rows_t, precision=hi)
    white_col = jnp.dot(lower_inv, gain_col_t, precision=hi)
    new_cov = cov - jnp.einsum("mi,mj->ij", white_row, white_col, precision=mid)
    coef = jax.scipy.linalg.cho_solve((lower, True), targets - pred_all)
    own_weights = lax.dynamic_slice_in_dim(weights.reshape(-1), device_id * blk, blk, 0)
    new_weights = own_weights + jnp.dot(coef, gain_own_t, precision=hi)
    return (new_weights, new_cov)


def solution(mesh):
    return jax.shard_map(
        on_device,
        mesh=mesh,
        in_specs=(
            P(("row", "col"), None),
            P(("row", "col")),
            P(("row", "col"), None),
            P(("row", "col")),
            P(),
            P(),
            P(),
            P(),
            P(),
            P("row", "col"),
        ),
        out_specs=(P(("row", "col")), P("row", "col")),
        check_vma=False,
    )
```

```python
import jax
import jax.numpy as jnp
from jax import lax
from jax.sharding import PartitionSpec as P

FR = 64


def broadcast_rows(buf, n_row, n_col, factor):
    bits = []
    b = 1
    while b < n_row:
        bits.append(b)
        b *= 2
    bits = bits[1:][::-1] + bits[:1]
    held = [0]
    for bit in bits:
        perm = []
        for c in range(n_col):
            s = c // factor
            for rel in held:
                perm.append(((s ^ rel) * n_col + c, (s ^ rel ^ bit) * n_col + c))
        buf = buf + lax.ppermute(buf, ("row", "col"), perm)
        held = held + [rel ^ bit for rel in held]
    return buf


def butterfly_sum(buf, axis, size):
    bit = 1
    while bit < size:
        buf = buf + lax.ppermute(buf, axis, [(i, i ^ bit) for i in range(size)])
        bit *= 2
    return buf


def halving_scatter(x, axis, size, me, done=0):
    nbits = size.bit_length() - 1
    for step in range(done, nbits):
        bit = 1 << step
        mine = (me // bit) % 2
        keep = lax.dynamic_index_in_dim(x, mine, 0, keepdims=False)
        send = lax.dynamic_index_in_dim(x, 1 - mine, 0, keepdims=False)
        x = keep + lax.ppermute(send, axis, [(i, i ^ bit) for i in range(size)])
    return x


def shift_all_to_all(x, axis, size, me):
    got = [lax.dynamic_index_in_dim(x, me, 1, keepdims=False)]
    for k in range(1, size):
        piece = lax.dynamic_index_in_dim(x, (me + size - k) % size, 1, keepdims=False)
        got.append(lax.ppermute(piece, axis, [(i, (i - k) % size) for i in range(size)]))
    got = jnp.stack(got, axis=0)
    both = jnp.concatenate([got, got], axis=0)
    ordered = lax.dynamic_slice_in_dim(both, (size - me) % size, size, 0)
    return ordered.reshape((size * x.shape[0],) + x.shape[2:])


def doubling_gather(x, axis, size, me):
    bits = []
    bit = 1
    while bit < size:
        bits.append(bit)
        bit *= 2
    rows = x.shape[0]
    x = x[None]
    for bit in bits[::-1]:
        other = lax.ppermute(x, axis, [(i, i ^ bit) for i in range(size)])
        low = (me // bit) % 2 == 0
        x = jnp.where(low, jnp.stack([x, other], axis=1), jnp.stack([other, x], axis=1))
        x = x.reshape((x.shape[0] * 2,) + x.shape[2:])
    return x.reshape((size * rows,) + x.shape[2:])


def on_device(
    atom_feat, types, neighbors, frame_of_atom, weights, type_gain, out_vec, targets, noise, cov
):
    hi = lax.Precision.HIGHEST
    mid = lax.Precision.HIGH
    atoms = atom_feat.shape[0]
    ntypes = type_gain.shape[0]
    nbrs = neighbors.shape[1]
    frames = atoms // FR
    onehot_type = (types[:, None] == jnp.arange(ntypes)[None, :]).astype(jnp.float32)
    row_gain = jnp.dot(onehot_type, type_gain, precision=hi)
    row_out = jnp.dot(onehot_type, out_vec, precision=hi)
    scaled = atom_feat * row_gain
    counts = jnp.sum(
        (neighbors[:, :, None] == jnp.arange(atoms)[None, None, :]).astype(jnp.float32), axis=1
    )
    near_sum = jnp.dot(counts, scaled, precision=hi)
    desc = jnp.tanh(atom_feat + near_sum / nbrs)
    act = jnp.tanh(jnp.dot(desc, weights, precision=hi))
    site_energy = jnp.sum(act * row_out, axis=1)
    slope = (1.0 - act * act) * row_out
    member = (frame_of_atom[:, None] == jnp.arange(frames)[None, :]).astype(jnp.float32)
    pred_local = jnp.dot(site_energy, member, precision=hi) / FR
    grads = jnp.einsum("af,ai,aj->fij", member, desc, slope, precision=hi) / FR
    width = grads.shape[1] * grads.shape[2]
    grads = grads.reshape(frames, width)
    n_row = lax.axis_size("row")
    n_col = lax.axis_size("col")
    row_id = lax.axis_index("row")
    col_id = lax.axis_index("col")
    m_all = frames * n_row * n_col
    col_w = width // n_col
    blk = width // (n_row * n_col)
    col_part = shift_all_to_all(grads.reshape(frames, n_col, col_w), "col", n_col, col_id)
    grad_col = doubling_gather(col_part.reshape(n_col * frames, col_w), "row", n_row, row_id)
    nbits = n_col.bit_length() - 1
    letters = "abcdefgh"[:nbits]
    cov_blocks = cov.reshape((2,) * nbits + (cov.shape[0] // n_col, cov.shape[1]))
    first = col_id % 2
    spec = "mk," + letters[:-1] + "ik->" + letters[:-1][::-1] + "mi"
    send_rows = lax.dynamic_index_in_dim(cov_blocks, 1 - first, nbits - 1, keepdims=False)
    send_part = jnp.einsum(spec, grad_col, send_rows, precision=mid)
    got_part = lax.ppermute(send_part, "col", [(i, i ^ 1) for i in range(n_col)])
    keep_rows = lax.dynamic_index_in_dim(cov_blocks, first, nbits - 1, keepdims=False)
    keep_part = jnp.einsum(spec, grad_col, keep_rows, precision=mid)
    partial_t = (keep_part, got_part)
    factor = n_col // n_row
    perm = []
    for r in range(n_row):
        for q in range(factor):
            for t in range(n_row):
                perm.append((t * n_col + r * factor + q, r * n_col + q * n_row + t))
    own_piece = lax.dynamic_slice_in_dim(grad_col, row_id * blk, blk, 1)
    grad_own = lax.ppermute(own_piece, ("row", "col"), perm)
    grad_own, keep_part = lax.optimization_barrier((grad_own, partial_t[0]))
    partial_t = keep_part + partial_t[1]
    gain_own_t = halving_scatter(partial_t, "col", n_col, col_id, 1)
    gram_own = jnp.einsum("mk,nk->mn", grad_own, gain_own_t, precision=hi)
    device_id = row_id * n_col + col_id
    slots = lax.dynamic_update_slice_in_dim(
        jnp.zeros((8, m_all), jnp.float32),
        jnp.zeros((8, frames), jnp.float32).at[0].set(pred_local),
        device_id * frames,
        1,
    )
    small = jnp.concatenate([gram_own, slots], axis=0)
    small = butterfly_sum(butterfly_sum(small, "col", n_col), "row", n_row)
    gain_rows_t = lax.all_gather(gain_own_t, "col", axis=1, tiled=True)
    gram = small[:m_all] + jnp.diag(noise)
    pred_all = small[m_all]
    lower = jnp.linalg.cholesky(gram)
    lower, gain_rows_t = lax.optimization_barrier((lower, gain_rows_t))
    half_t = lax.dynamic_slice_in_dim(gain_rows_t, col_id % factor * col_w, col_w, 1)
    mine = row_id == col_id // factor
    masked = jnp.where(mine, half_t, jnp.zeros_like(half_t))
    gain_col_t = broadcast_rows(masked, n_row, n_col, factor)
    white_row = jax.scipy.linalg.solve_triangular(lower, gain_rows_t, lower=True)
    white_col = jax.scipy.linalg.solve_triangular(lower, gain_col_t, lower=True)
    new_cov = cov - jnp.einsum("mi,mj->ij", white_row, white_col, precision=mid)
    coef = jax.scipy.linalg.cho_solve((lower, True), targets - pred_all)
    own_weights = lax.dynamic_slice_in_dim(weights.reshape(-1), device_id * blk, blk, 0)
    new_weights = own_weights + jnp.dot(coef, gain_own_t, precision=hi)
    return (new_weights, new_cov)


def solution(mesh):
    return jax.shard_map(
        on_device,
        mesh=mesh,
        in_specs=(
            P(("row", "col"), None),
            P(("row", "col")),
            P(("row", "col"), None),
            P(("row", "col")),
            P(),
            P(),
            P(),
            P(),
            P(),
            P("row", "col"),
        ),
        out_specs=(P(("row", "col")), P("row", "col")),
        check_vma=False,
    )
```

```python
import jax
import jax.numpy as jnp
from jax import lax
from jax.sharding import PartitionSpec as P

FR = 64


def broadcast_rows(buf, n_row, n_col, factor):
    bits = []
    b = 1
    while b < n_row:
        bits.append(b)
        b *= 2
    bits = bits[1:][::-1] + bits[:1]
    held = [0]
    for bit in bits:
        perm = []
        for c in range(n_col):
            s = c // factor
            for rel in held:
                perm.append(((s ^ rel) * n_col + c, (s ^ rel ^ bit) * n_col + c))
        buf = buf + lax.ppermute(buf, ("row", "col"), perm)
        held = held + [rel ^ bit for rel in held]
    return buf


def butterfly_sum(buf, axis, size):
    bit = 1
    while bit < size:
        buf = buf + lax.ppermute(buf, axis, [(i, i ^ bit) for i in range(size)])
        bit *= 2
    return buf


def halving_scatter(x, axis, size, me, done=0):
    nbits = size.bit_length() - 1
    for step in range(done, nbits):
        bit = 1 << step
        mine = (me // bit) % 2
        keep = lax.dynamic_index_in_dim(x, mine, 0, keepdims=False)
        send = lax.dynamic_index_in_dim(x, 1 - mine, 0, keepdims=False)
        x = keep + lax.ppermute(send, axis, [(i, i ^ bit) for i in range(size)])
    return x


def shift_all_to_all(x, axis, size, me):
    got = [lax.dynamic_index_in_dim(x, me, 1, keepdims=False)]
    for k in range(1, size):
        piece = lax.dynamic_index_in_dim(x, (me + size - k) % size, 1, keepdims=False)
        got.append(lax.ppermute(piece, axis, [(i, (i - k) % size) for i in range(size)]))
    got = jnp.stack(got, axis=0)
    both = jnp.concatenate([got, got], axis=0)
    ordered = lax.dynamic_slice_in_dim(both, (size - me) % size, size, 0)
    return ordered.reshape((size * x.shape[0],) + x.shape[2:])


def doubling_gather(x, axis, size, me):
    bits = []
    bit = 1
    while bit < size:
        bits.append(bit)
        bit *= 2
    rows = x.shape[0]
    x = x[None]
    for bit in bits[::-1]:
        other = lax.ppermute(x, axis, [(i, i ^ bit) for i in range(size)])
        low = (me // bit) % 2 == 0
        x = jnp.where(low, jnp.stack([x, other], axis=1), jnp.stack([other, x], axis=1))
        x = x.reshape((x.shape[0] * 2,) + x.shape[2:])
    return x.reshape((size * rows,) + x.shape[2:])


def on_device(
    atom_feat, types, neighbors, frame_of_atom, weights, type_gain, out_vec, targets, noise, cov
):
    hi = lax.Precision.HIGHEST
    mid = lax.Precision.HIGH
    atoms = atom_feat.shape[0]
    ntypes = type_gain.shape[0]
    nbrs = neighbors.shape[1]
    frames = atoms // FR
    onehot_type = (types[:, None] == jnp.arange(ntypes)[None, :]).astype(jnp.float32)
    row_gain = jnp.dot(onehot_type, type_gain, precision=hi)
    row_out = jnp.dot(onehot_type, out_vec, precision=hi)
    scaled = atom_feat * row_gain
    counts = jnp.sum(
        (neighbors.T[:, :, None] == jnp.arange(atoms)[None, None, :]).astype(jnp.float32), axis=0
    )
    near_sum = jnp.dot(counts, scaled, precision=hi)
    desc = jnp.tanh(atom_feat + near_sum / nbrs)
    act = jnp.tanh(jnp.dot(desc, weights, precision=hi))
    site_energy = jnp.sum(act * row_out, axis=1)
    slope = (1.0 - act * act) * row_out
    member = (frame_of_atom[:, None] == jnp.arange(frames)[None, :]).astype(jnp.float32)
    pred_local = jnp.dot(site_energy, member, precision=hi) / FR
    grads = jnp.einsum("af,ai,aj->fij", member, desc, slope, precision=hi) / FR
    width = grads.shape[1] * grads.shape[2]
    grads = grads.reshape(frames, width)
    n_row = lax.axis_size("row")
    n_col = lax.axis_size("col")
    row_id = lax.axis_index("row")
    col_id = lax.axis_index("col")
    m_all = frames * n_row * n_col
    col_w = width // n_col
    blk = width // (n_row * n_col)
    col_part = shift_all_to_all(grads.reshape(frames, n_col, col_w), "col", n_col, col_id)
    grad_col = doubling_gather(col_part.reshape(n_col * frames, col_w), "row", n_row, row_id)
    nbits = n_col.bit_length() - 1
    letters = "abcdefgh"[:nbits]
    cov_blocks = cov.reshape((2,) * nbits + (cov.shape[0] // n_col, cov.shape[1]))
    first = col_id % 2
    spec = "mk," + letters[:-1] + "ik->" + letters[:-1][::-1] + "mi"
    send_rows = lax.dynamic_index_in_dim(cov_blocks, 1 - first, nbits - 1, keepdims=False)
    send_part = jnp.einsum(spec, grad_col, send_rows, precision=mid)
    got_part = lax.ppermute(send_part, "col", [(i, i ^ 1) for i in range(n_col)])
    keep_rows = lax.dynamic_index_in_dim(cov_blocks, first, nbits - 1, keepdims=False)
    keep_part = jnp.einsum(spec, grad_col, keep_rows, precision=mid)
    partial_t = (keep_part, got_part)
    factor = n_col // n_row
    grad_own = None
    for t in range(n_row):
        perm = []
        for r in range(n_row):
            for q in range(factor):
                perm.append((r * n_col + r * factor + q, r * n_col + q * n_row + t))
        got = lax.ppermute(grad_col[:, t * blk : (t + 1) * blk], ("row", "col"), perm)
        grad_own = got if grad_own is None else grad_own + got
    grad_own, keep_part = lax.optimization_barrier((grad_own, partial_t[0]))
    partial_t = keep_part + partial_t[1]
    gain_own_t = halving_scatter(partial_t, "col", n_col, col_id, 1)
    gram_own = jnp.einsum("mk,nk->mn", grad_own, gain_own_t, precision=hi)
    device_id = row_id * n_col + col_id
    slots = lax.dynamic_update_slice_in_dim(
        jnp.zeros((8, m_all), jnp.float32),
        jnp.zeros((8, frames), jnp.float32).at[0].set(pred_local),
        device_id * frames,
        1,
    )
    small = jnp.concatenate([gram_own, slots], axis=0)
    small = butterfly_sum(butterfly_sum(small, "col", n_col), "row", n_row)
    gain_rows_t = lax.all_gather(gain_own_t, "col", axis=1, tiled=True)
    gram = small[:m_all] + jnp.diag(noise)
    pred_all = small[m_all]
    lower = jnp.linalg.cholesky(gram)
    lower, gain_rows_t = lax.optimization_barrier((lower, gain_rows_t))
    half_t = lax.dynamic_slice_in_dim(gain_rows_t, col_id % factor * col_w, col_w, 1)
    mine = row_id == col_id // factor
    masked = jnp.where(mine, half_t, jnp.zeros_like(half_t))
    gain_col_t = broadcast_rows(masked, n_row, n_col, factor)
    white_row = jax.scipy.linalg.solve_triangular(lower, gain_rows_t, lower=True)
    white_col = jax.scipy.linalg.solve_triangular(lower, gain_col_t, lower=True)
    new_cov = cov - jnp.einsum("mi,mj->ij", white_row, white_col, precision=mid)
    coef = jax.scipy.linalg.cho_solve((lower, True), targets - pred_all)
    own_weights = lax.dynamic_slice_in_dim(weights.reshape(-1), device_id * blk, blk, 0)
    new_weights = own_weights + jnp.dot(coef, gain_own_t, precision=hi)
    return (new_weights, new_cov)


def solution(mesh):
    return jax.shard_map(
        on_device,
        mesh=mesh,
        in_specs=(
            P(("row", "col"), None),
            P(("row", "col")),
            P(("row", "col"), None),
            P(("row", "col")),
            P(),
            P(),
            P(),
            P(),
            P(),
            P("row", "col"),
        ),
        out_specs=(P(("row", "col")), P("row", "col")),
        check_vma=False,
    )
```
